128 devices in a mesh: seq: 16 (over x_hi, z, core), tensor: 8 (over y, x_lo).
Axes of the slice: x: 4 (x_hi: 2, x_lo: 2; x = x_hi * 2 + x_lo), y: 4, z: 4, core: 2. Of those that a mesh axis runs over, the one named last changes fastest.
Arguments:
- layer_input: bfloat16 [16384, 1024], P('seq'), may hold values from -3 to 3
- queries: bfloat16 [16384, 1024], P('seq', 'tensor'), may hold values from -2.5 to 2.5
- fresh_keys: bfloat16 [16384, 1024], P('seq', 'tensor'), may hold values from -3 to 3
- fresh_values: bfloat16 [16384, 1024], P('seq', 'tensor'), may hold values from -6 to 6
- cached_keys: bfloat16 [12288, 1024], P('seq', 'tensor'), may hold values from -2.5 to 2.5
- cached_values: bfloat16 [12288, 1024], P('seq', 'tensor'), may hold values from -6 to 6
- start_position: int32 [1], replicated, may hold values from 12288 to 12383
- bias_table: float32 [32, 16], P(None, 'tensor'), may hold values from -4 to 4
- out_weight: bfloat16 [1024, 1024], P('tensor'), may hold values from -0.1875 to 0.1875
- norm_gain: float32 [1024], replicated, may hold values from 0.1 to 1.9
- routes: int32 [16384, 2], P('seq'), may hold values from 0 to 7, all different within a row; in each aligned block of 1024 rows (0 to 1023, 1024 to 2047, ...) at most 384 rows name the same one
- route_weights: float32 [16384, 2], P('seq'), may hold values from 0.2 to 1
- expert_in: bfloat16 [8, 1024, 2, 2816], P(None, None, None, 'tensor'), may hold values from -0.1875 to 0.1875
- expert_out: bfloat16 [8, 2816, 1024], P(None, 'tensor'), may hold values from -0.109375 to 0.109375
Outputs:
- mixed: bfloat16 [16384, 1024], P('seq', 'tensor')
The draws below stay inside these ranges and needn't reach their ends.
Inputs may be any that keep to these rules, and one draw needn't show every extreme that they name: `routes`: in the rows of one device (aligned blocks of 1024 rows) no expert is named more than 384 times; some expert reaches 384 in every draw. A row names 2 different experts.
All inputs are finite; a program needn't handle non-finite values.
Results may differ from the reference program's by a relative error of at most 0.019.
Values may be sent and summed in bfloat16 or wider, within the bound.
No kernel may reach another device: no remote copies, remote signals or barrier semaphores. Data moves between devices by JAX's collectives and lax.ppermute only.
A program may use at most 192 MiB of HBM per device.

```python
import math
import jax
import jax.numpy as jnp
import numpy as np
from jax import lax

D = 1024
HEADS = 16
HEAD_DIM = 64
FF = 2816
EXPERTS = 8
TOP = 2
BUCKETS = 32
TOK_DEV = 1024
CAP = 384
TOKENS = 16384
PRIOR = 12288
N_SEQ = 16


def draw_queries(key, part):
    values = jax.random.normal(jax.random.fold_in(key, 11), (TOKENS, HEADS * HEAD_DIM), jnp.float32) * 0.5
    values = jnp.clip(values, -2.5, 2.5)
    return values.astype(jnp.bfloat16)


def draw_cached_keys(key, part):
    values = jax.random.normal(jax.random.fold_in(key, 23), (PRIOR, HEADS * HEAD_DIM), jnp.float32) * 0.5
    values = jnp.clip(values, -2.5, 2.5)
    return values.astype(jnp.bfloat16)


def steps_of(stream_key, extent, pieces, least, top_value):
    factor_of = 1.0
    for axis_at, blocks in pieces:
        heights = jax.random.uniform(jax.random.fold_in(jax.random.fold_in(stream_key, 6), axis_at), (blocks,), jnp.float32, least / len(pieces), top_value / len(pieces))
        factor_of = factor_of * jnp.repeat(jnp.exp(heights), extent[axis_at] // blocks).reshape((-1,) + (1,) * (len(extent) - 1 - axis_at))
    return factor_of


def shared_out(key, own, number, rows, count, top, limit, slope):
    order = jax.random.permutation(key, count)
    packed, common = load_shares(count, rows * top, limit, slope, True), load_shares(count, rows * top, limit, slope, False)
    places = jnp.arange(count)

    def named(lengths, rotation):
        used = int((lengths > 0).sum())
        fixed = max(1, used // 4)
        moved = fixed + (places - fixed + rotation * (used - fixed)) % max(1, count - fixed)
        return jnp.zeros((count,), jnp.int32).at[order[jnp.where(places < fixed, places, moved)]].set(jnp.asarray(lengths, jnp.int32))

    lengths = jnp.where(number % 4 == 0, named(packed, number // 4), named(common, number - number // 4 - 1))
    mixed = jax.random.permutation(jax.random.fold_in(own, 3), count)
    source_of, sink = mixed[0:count // 2 * 2:2], mixed[1:count // 2 * 2:2]
    room = jnp.minimum(lengths[source_of] - 1, limit - lengths[sink]) // 2
    room = jnp.where((source_of == order[0]) | (sink == order[0]) | (lengths[sink] == 0), 0, jnp.maximum(room, 0))
    moved = jax.random.randint(jax.random.fold_in(own, 4), (count // 2,), 0, 1 << 20) % (room + 1)
    lengths = lengths.at[source_of].add(-moved).at[sink].add(moved)
    labels = jnp.searchsorted(jnp.cumsum(lengths), jnp.arange(rows * top), side="right").astype(jnp.int32)
    table = labels.reshape(top, rows).T
    table = table[jax.random.permutation(jax.random.fold_in(own, 1), rows)]
    rotation = jax.random.randint(jax.random.fold_in(own, 2), (rows, 1), 0, top)
    return jnp.take_along_axis(table, (jnp.arange(top)[None, :] + rotation) % top, axis=1)


def load_shares(number_of, total, limit, lean, full):
    loads = [(1 << 20) // math.isqrt(rank ** lean) + 1 for rank in range(1, number_of + 1)]
    largest = limit if full else min(limit, max(-(-total // number_of), total * loads[0] // sum(loads)))
    least = 1 if total - largest >= number_of - 1 else 0
    holding, surplus = [largest] + [least] * (number_of - 1), total - largest - least * (number_of - 1)
    while surplus > 0:
        candidates = [i for i in range(1, number_of) if holding[i] < largest] or [i for i in range(1, number_of) if holding[i] < limit]
        mass, left = sum([loads[i] for i in candidates]), surplus
        for i in candidates:
            extra = min(limit - holding[i], max(1, left * loads[i] // mass), surplus)
            holding[i] = holding[i] + extra
            surplus = surplus - extra
    return np.array(holding)


def scatter_about(rng, shape, deviation, most, split=(), kind=jnp.bfloat16):
    values = jax.random.normal(rng, shape, jnp.float32) * deviation
    if len(split) > 0:
        values = steps_of(rng, shape, split, -0.22, 0.18) * values
    return jnp.clip(values, min=-most, max=most).astype(kind)


def setup_inputs(seed: int = 0) -> dict:
    key_list = jax.random.split(jax.random.key(seed), 15)
    layer_input = scatter_about(key_list[0], (TOKENS, D), 0.5, 3.0, ((0, 16),))
    queries = draw_queries(jax.random.fold_in(key_list[14], 71), 0)
    fresh_keys = scatter_about(key_list[2], (TOKENS, HEADS * HEAD_DIM), 0.5, 3.0, ((0, 16), (1, 8)))
    fresh_values = scatter_about(key_list[3], (TOKENS, HEADS * HEAD_DIM), 1.0, 6.0, ((0, 16), (1, 8)))
    cached_keys = draw_cached_keys(jax.random.fold_in(key_list[14], 71), 0)
    cached_values = scatter_about(key_list[5], (PRIOR, HEADS * HEAD_DIM), 1.0, 6.0, ((0, 16), (1, 8)))
    start_position = jax.random.randint(key_list[6], (1,), PRIOR, PRIOR + 96).astype(jnp.int32)
    bias_table = scatter_about(key_list[7], (BUCKETS, HEADS), 1.0, 4.0, ((1, 8),), jnp.float32)
    out_weight = scatter_about(key_list[8], (HEADS * HEAD_DIM, D), (HEADS * HEAD_DIM) ** -0.5, 0.1875, ((0, 8),))
    norm_gain = jnp.clip(1.0 + 0.18 * jax.random.normal(key_list[9], (D,), jnp.float32), 0.1, 1.9)
    routes_keys = jax.random.split(jax.random.fold_in(key_list[10], 1), TOKENS // TOK_DEV)
    routes_turns = jax.random.permutation(jax.random.fold_in(key_list[10], 3), TOKENS // TOK_DEV)
    routes = jax.vmap(lambda own, number: shared_out(jax.random.fold_in(key_list[10], 2), own, number, TOK_DEV, EXPERTS, TOP, CAP, 2))(routes_keys, routes_turns).reshape((TOKENS, TOP))
    route_weights = jnp.clip(0.2 + 0.8 * jax.random.uniform(key_list[11], (TOKENS, TOP), jnp.float32) ** steps_of(key_list[11], (TOKENS, TOP), ((0, 16),), -0.2, 0.2), 0.2, 1.0)
    expert_in = scatter_about(key_list[12], (EXPERTS, D, 2, FF), D ** -0.5, 0.1875, ((3, 8),))
    expert_out = scatter_about(key_list[13], (EXPERTS, FF, D), FF ** -0.5, 0.109375, ((1, 8),))
    return dict(layer_input=layer_input, queries=queries, fresh_keys=fresh_keys, fresh_values=fresh_values, cached_keys=cached_keys, cached_values=cached_values, start_position=start_position, bias_table=bias_table, out_weight=out_weight, norm_gain=norm_gain, routes=routes, route_weights=route_weights, expert_in=expert_in, expert_out=expert_out)


bucket_edges = [edge for edge in range(1, 17)] + [math.ceil(16 * 8 ** (level / 16)) for level in range(1, 16)]

def bucket_of(distance):
    clipped = jnp.maximum(distance, 0)
    bucket = jnp.zeros(clipped.shape, jnp.int32)
    for edge in bucket_edges:
        bucket = bucket + (clipped >= edge).astype(jnp.int32)
    return bucket

def reference(layer_input, queries, fresh_keys, fresh_values, cached_keys, cached_values, start_position, bias_table, out_weight, norm_gain, routes, route_weights, expert_in, expert_out):
    offset = start_position[0].astype(jnp.int32)
    key_rows = jnp.concatenate([cached_keys, fresh_keys], 0)
    value_rows = jnp.concatenate([cached_values, fresh_values], 0)
    key_pos = jnp.concatenate([jnp.arange(PRIOR, dtype=jnp.int32), offset + jnp.arange(TOKENS, dtype=jnp.int32)])
    row_block = math.gcd(TOKENS, 512)
    block_count = TOKENS // row_block

    def one_block(number):
        first_row = (number * row_block).astype(jnp.int32)
        query_rows = lax.dynamic_slice_in_dim(queries, first_row, row_block, 0)
        query_pos = offset + first_row + jnp.arange(row_block, dtype=jnp.int32)
        distance = query_pos[:, None] - key_pos[None, :]
        bucket = bucket_of(distance)
        allowed = distance >= 0

        def one_head(head):
            column = (head * HEAD_DIM).astype(jnp.int32)
            head_q = lax.dynamic_slice_in_dim(query_rows, column, HEAD_DIM, 1)
            head_k = lax.dynamic_slice_in_dim(key_rows, column, HEAD_DIM, 1)
            head_v = lax.dynamic_slice_in_dim(value_rows, column, HEAD_DIM, 1)
            table_column = lax.dynamic_index_in_dim(bias_table, head, 1, keepdims=False)
            scores = jnp.dot(head_q, head_k.T, preferred_element_type=jnp.float32)
            scores = scores + jnp.take(table_column, bucket)
            scores = jnp.where(allowed, scores, -jnp.inf)
            maxima = lax.optimization_barrier(jnp.max(scores, axis=-1))
            expon = jnp.exp(scores - maxima[:, None])
            totals = lax.optimization_barrier(jnp.sum(expon, axis=-1))
            weighted = jnp.dot(expon.astype(jnp.bfloat16), head_v, preferred_element_type=jnp.float32)
            return (weighted / totals[:, None]).astype(jnp.bfloat16)
        heads_out = lax.map(one_head, jnp.arange(HEADS, dtype=jnp.int32))
        return jnp.transpose(heads_out, (1, 0, 2)).reshape(row_block, HEADS * HEAD_DIM)
    attended = lax.map(one_block, jnp.arange(block_count, dtype=jnp.int32)).reshape(TOKENS, HEADS * HEAD_DIM)
    resid = layer_input.astype(jnp.float32) + jnp.dot(attended, out_weight, preferred_element_type=jnp.float32)
    normed = (resid * lax.rsqrt(lax.optimization_barrier(jnp.mean(resid * resid, axis=-1, keepdims=True)) + 1e-06) * norm_gain).astype(jnp.bfloat16)
    slots_all = CAP * N_SEQ
    flat_routes = routes.reshape(-1)
    onehot = (flat_routes[:, None] == jnp.arange(EXPERTS, dtype=jnp.int32)[None, :]).astype(jnp.int32)
    before = jnp.cumsum(onehot, axis=0) - onehot
    slot = lax.optimization_barrier(jnp.sum(before * onehot, axis=1))
    target = flat_routes * slots_all + slot
    owner = jnp.arange(TOKENS * TOP, dtype=jnp.int32) // TOP
    slot_owner = jnp.zeros((EXPERTS * slots_all,), jnp.int32).at[target].set(owner)
    buffer = jnp.take(normed, slot_owner, axis=0).reshape(EXPERTS, slots_all, D)

    def one_expert(expert):
        rows_here = lax.dynamic_index_in_dim(buffer, expert, 0, keepdims=False)
        weight_in = lax.dynamic_index_in_dim(expert_in, expert, 0, keepdims=False).reshape(D, 2 * FF)
        weight_out = lax.dynamic_index_in_dim(expert_out, expert, 0, keepdims=False)
        gate_up = jnp.dot(rows_here, weight_in, preferred_element_type=jnp.float32).reshape(slots_all, 2, FF)
        hidden = (jax.nn.gelu(gate_up[:, 0], approximate=True) * gate_up[:, 1]).astype(jnp.bfloat16)
        return jnp.dot(hidden, weight_out, preferred_element_type=jnp.float32)
    expert_rows = lax.map(one_expert, jnp.arange(EXPERTS, dtype=jnp.int32)).reshape(EXPERTS * slots_all, D)
    picked = jnp.take(expert_rows, target, axis=0).reshape(TOKENS, TOP, D)
    combined = lax.optimization_barrier(jnp.sum(picked * route_weights[:, :, None], axis=1))
    return (resid + combined).astype(jnp.bfloat16)
```

```python
import math

import jax
import jax.numpy as jnp
from jax import lax
from jax.experimental import pallas as pl
from jax.experimental.pallas import tpu as pltpu
from jax.sharding import PartitionSpec as P

D = 1024
HEAD_DIM = 64
TOP = 2
CAP = 384
KEY_TILE = 512
ROW_BLOCK = 128


bucket_edges = [edge for edge in range(1, 17)] + [
    math.ceil(16 * 8 ** (level / 16)) for level in range(1, 16)
]
far_edge = bucket_edges[-1]
epsilon = 1e-06
lowest = -1e30


def attn_kernel(scal_ref, dtab_ref, q_ref, k_ref, v_ref, m_in, l_in, acc_in, m_ref, l_ref, acc_ref):
    t = pl.program_id(0)
    tk = k_ref.shape[0]
    rows_all = q_ref.shape[0]

    @pl.when(t == 0)
    def _():
        m_ref[...] = m_in[...]
        l_ref[...] = l_in[...]
        acc_ref[...] = acc_in[...]

    qk_off = scal_ref[0]
    n_valid = scal_ref[1]

    def update(r, near):
        rows = pl.ds(r * ROW_BLOCK, ROW_BLOCK)
        q = q_ref[rows, :]
        k = k_ref[...]
        v = v_ref[...]
        lane = lax.broadcasted_iota(jnp.int32, (1, q.shape[1]), 1) < HEAD_DIM
        zero_q = jnp.zeros_like(q)
        if near:
            base = qk_off + r * ROW_BLOCK - t * tk
            d = (
                base
                + lax.broadcasted_iota(jnp.int32, (ROW_BLOCK, tk), 0)
                - lax.broadcasted_iota(jnp.int32, (ROW_BLOCK, tk), 1)
            )
            allowed = d >= 0
            bucket = jnp.zeros(d.shape, jnp.int32)
            for edge in bucket_edges:
                bucket = bucket + (d >= edge).astype(jnp.int32)
        news = []
        alphas = []
        pvs = []
        for h in range(2):
            qh = jnp.where(lane, q, zero_q) if h == 0 else jnp.where(lane, zero_q, q)
            s = lax.dot_general(
                qh, k, (((1,), (1,)), ((), ())), preferred_element_type=jnp.float32
            )
            if near:
                delta = jnp.zeros(s.shape, jnp.float32)
                for level in range(len(bucket_edges)):
                    delta = jnp.where(bucket == level, dtab_ref[level, h], delta)
                s = jnp.where(allowed, s + delta, -jnp.inf)
            m_prev = m_ref[h, rows, :]
            m_curr = jnp.max(s, axis=1, keepdims=True)
            m_next = jnp.maximum(m_prev, m_curr)
            p = jnp.exp(s - jnp.tile(m_next, (1, tk // m_next.shape[1])))
            alpha = jnp.exp(m_prev - m_next)
            l_ref[h, rows, :] = alpha * l_ref[h, rows, :] + jnp.sum(p, axis=1, keepdims=True)
            m_ref[h, rows, :] = m_next
            pv = jnp.dot(p.astype(v.dtype), v, preferred_element_type=jnp.float32)
            alphas.append(alpha)
            pvs.append(pv)
        alpha_b = jnp.where(lane, alphas[0], alphas[1])
        pv_b = jnp.where(lane, pvs[0], pvs[1])
        acc_ref[rows, :] = alpha_b * acc_ref[rows, :] + pv_b

    @pl.when(t < n_valid)
    def _():
        for r in range(rows_all // ROW_BLOCK):
            dmin = qk_off + r * ROW_BLOCK - (t * tk + tk - 1)
            dmax = qk_off + r * ROW_BLOCK + ROW_BLOCK - 1 - t * tk

            @pl.when(dmin >= far_edge)
            def _():
                update(r, False)

            @pl.when((dmin < far_edge) & (dmax >= 0))
            def _():
                update(r, True)


def attend(state, q, keys, values, qk_off, n_valid, dtab):
    m, l, acc = state
    rows, width = q.shape
    n_tiles = keys.shape[0] // KEY_TILE
    scal = jnp.stack([qk_off.astype(jnp.int32), n_valid.astype(jnp.int32)])

    def tile_map(t, sc):
        return (jnp.maximum(jnp.minimum(t, sc[1] - 1), 0), 0)

    full2 = lambda t, sc: (0, 0)
    full3 = lambda t, sc: (0, 0, 0)
    flops = 8 * rows * KEY_TILE * width * n_tiles * 2
    cost = pl.CostEstimate(
        flops=flops,
        transcendentals=2 * rows * KEY_TILE * n_tiles,
        bytes_accessed=2 * keys.size * 2 + 6 * rows * width * 4,
    )
    return pl.pallas_call(
        attn_kernel,
        out_shape=(
            jax.ShapeDtypeStruct(m.shape, jnp.float32),
            jax.ShapeDtypeStruct(l.shape, jnp.float32),
            jax.ShapeDtypeStruct(acc.shape, jnp.float32),
        ),
        grid_spec=pltpu.PrefetchScalarGridSpec(
            num_scalar_prefetch=1,
            grid=(n_tiles,),
            in_specs=[
                pl.BlockSpec(memory_space=pltpu.SMEM),
                pl.BlockSpec((rows, width), full2),
                pl.BlockSpec((KEY_TILE, width), tile_map),
                pl.BlockSpec((KEY_TILE, width), tile_map),
                pl.BlockSpec(m.shape, full3),
                pl.BlockSpec(l.shape, full3),
                pl.BlockSpec(acc.shape, full2),
            ],
            out_specs=[
                pl.BlockSpec(m.shape, full3),
                pl.BlockSpec(l.shape, full3),
                pl.BlockSpec(acc.shape, full2),
            ],
        ),
        compiler_params=pltpu.CompilerParams(dimension_semantics=("arbitrary",)),
        cost_estimate=cost,
    )(scal, dtab, q, keys, values, m, l, acc)


def rms_scale(rows, gain):
    return (
        rows * lax.rsqrt(jnp.mean(rows * rows, axis=-1, keepdims=True) + epsilon) * gain
    ).astype(jnp.bfloat16)


def per_device(
    layer_input,
    queries,
    fresh_keys,
    fresh_values,
    cached_keys,
    cached_values,
    start_position,
    bias_table,
    out_weight,
    norm_gain,
    routes,
    route_weights,
    expert_in,
    expert_out,
):
    tok_rows = queries.shape[0]
    width = queries.shape[1]
    offset = start_position[0]
    seq_index = lax.axis_index("seq")
    dtab = bias_table - bias_table[bias_table.shape[0] - 1][None, :]
    state = (
        jnp.full((2, tok_rows, 128), lowest, jnp.float32),
        jnp.zeros((2, tok_rows, 128), jnp.float32),
        jnp.zeros((tok_rows, width), jnp.float32),
    )
    own_tiles = fresh_keys.shape[0] // KEY_TILE
    state = attend(
        state, queries, fresh_keys, fresh_values, jnp.int32(0), jnp.int32(own_tiles), dtab
    )
    prior_k = lax.all_gather(cached_keys, "seq", axis=0, tiled=True)
    prior_v = lax.all_gather(cached_values, "seq", axis=0, tiled=True)
    state = attend(
        state,
        queries,
        prior_k,
        prior_v,
        offset + seq_index * tok_rows,
        jnp.int32(prior_k.shape[0] // KEY_TILE),
        dtab,
    )
    all_k = lax.all_gather(fresh_keys, "seq", axis=0, tiled=True)
    all_v = lax.all_gather(fresh_values, "seq", axis=0, tiled=True)
    state = attend(
        state,
        queries,
        all_k,
        all_v,
        seq_index * tok_rows,
        seq_index * own_tiles,
        dtab,
    )
    m, l, acc = state
    lane = lax.broadcasted_iota(jnp.int32, (1, width), 1) < HEAD_DIM
    totals = jnp.where(lane, l[0], l[1])
    attended = (acc / totals).astype(jnp.bfloat16)
    attended_full = lax.all_gather(attended, "tensor", axis=1, tiled=True)
    weight_full = lax.all_gather(out_weight, "tensor", axis=0, tiled=True)
    col_width = D // lax.axis_size("tensor")
    col_start = lax.axis_index("tensor") * col_width
    resid = layer_input.astype(jnp.float32) + jnp.dot(
        attended_full, weight_full, preferred_element_type=jnp.float32
    )
    normed = rms_scale(resid, norm_gain)
    resid_cols = lax.dynamic_slice_in_dim(resid, col_start, col_width, 1)
    expert_count = expert_in.shape[0]
    flat_routes = routes.reshape(-1)
    onehot = (flat_routes[:, None] == jnp.arange(expert_count, dtype=jnp.int32)[None, :]).astype(
        jnp.int32
    )
    before = jnp.cumsum(onehot, axis=0) - onehot
    slot = jnp.sum(before * onehot, axis=1)
    target = flat_routes * CAP + slot
    owner = jnp.arange(flat_routes.shape[0], dtype=jnp.int32) // TOP
    slot_owner = jnp.zeros((expert_count * CAP,), jnp.int32).at[target].set(owner)
    buffer = jnp.take(normed, slot_owner, axis=0).reshape(expert_count, CAP, D)
    gate_up = jnp.einsum("ecd,edgf->ecgf", buffer, expert_in, preferred_element_type=jnp.float32)
    hidden = (jax.nn.gelu(gate_up[:, :, 0], approximate=True) * gate_up[:, :, 1]).astype(
        jnp.bfloat16
    )
    expert_rows = jnp.einsum(
        "ecf,efd->ecd", hidden, expert_out, preferred_element_type=jnp.float32
    ).reshape(expert_count * CAP, D)
    picked = jnp.take(expert_rows, target, axis=0).reshape(tok_rows, TOP, D)
    combined = jnp.sum(picked * route_weights[:, :, None], axis=1)
    expert_cols = lax.psum_scatter(
        combined.astype(jnp.bfloat16), "tensor", scatter_dimension=1, tiled=True
    ).astype(jnp.float32)
    return (resid_cols + expert_cols).astype(jnp.bfloat16)


def solution(mesh):
    return jax.shard_map(
        per_device,
        mesh=mesh,
        in_specs=(
            P("seq", None),
            P("seq", "tensor"),
            P("seq", "tensor"),
            P("seq", "tensor"),
            P("seq", "tensor"),
            P("seq", "tensor"),
            P(),
            P(None, "tensor"),
            P("tensor", None),
            P(),
            P("seq", None),
            P("seq", None),
            P(None, None, None, "tensor"),
            P(None, "tensor", None),
        ),
        out_specs=P("seq", "tensor"),
        check_vma=False,
    )
```

```python
import math

import jax
import jax.numpy as jnp
from jax import lax
from jax.experimental import pallas as pl
from jax.experimental.pallas import tpu as pltpu
from jax.sharding import PartitionSpec as P

D = 1024
HEAD_DIM = 64
TOP = 2
CAP = 384
KEY_TILE = 512
ROW_BLOCK = 128


bucket_edges = [edge for edge in range(1, 17)] + [
    math.ceil(16 * 8 ** (level / 16)) for level in range(1, 16)
]
far_edge = bucket_edges[-1]
epsilon = 1e-06
lowest = -1e30


def attn_kernel(scal_ref, dtab_ref, q_ref, k_ref, v_ref, m_in, l_in, acc_in, m_ref, l_ref, acc_ref):
    t = pl.program_id(0)
    tk = k_ref.shape[0]
    rows_all = q_ref.shape[0]

    @pl.when(t == 0)
    def _():
        m_ref[...] = m_in[...]
        l_ref[...] = l_in[...]
        acc_ref[...] = acc_in[...]

    n_valid = scal_ref[2]
    active = (t < n_valid) & ((t < scal_ref[3]) | (t >= scal_ref[4]))
    half_blocks = rows_all // ROW_BLOCK // 2

    def update(r, near, qk_off):
        rows = pl.ds(r * ROW_BLOCK, ROW_BLOCK)
        q = q_ref[rows, :]
        k = k_ref[...]
        v = v_ref[...]
        lane = lax.broadcasted_iota(jnp.int32, (1, q.shape[1]), 1) < HEAD_DIM
        zero_q = jnp.zeros_like(q)
        if near:
            base = qk_off + r * ROW_BLOCK - t * tk
            d = (
                base
                + lax.broadcasted_iota(jnp.int32, (ROW_BLOCK, tk), 0)
                - lax.broadcasted_iota(jnp.int32, (ROW_BLOCK, tk), 1)
            )
            allowed = d >= 0
            bucket = jnp.zeros(d.shape, jnp.int32)
            for edge in bucket_edges:
                bucket = bucket + (d >= edge).astype(jnp.int32)
        news = []
        alphas = []
        pvs = []
        for h in range(2):
            qh = jnp.where(lane, q, zero_q) if h == 0 else jnp.where(lane, zero_q, q)
            s = lax.dot_general(
                qh, k, (((1,), (1,)), ((), ())), preferred_element_type=jnp.float32
            )
            if near:
                delta = jnp.zeros(s.shape, jnp.float32)
                for level in range(len(bucket_edges)):
                    delta = jnp.where(bucket == level, dtab_ref[level, h], delta)
                s = jnp.where(allowed, s + delta, -jnp.inf)
            m_prev = m_ref[h, rows, :]
            m_curr = jnp.max(s, axis=1, keepdims=True)
            m_next = jnp.maximum(m_prev, m_curr)
            p = jnp.exp(s - jnp.tile(m_next, (1, tk // m_next.shape[1])))
            alpha = jnp.exp(m_prev - m_next)
            l_ref[h, rows, :] = alpha * l_ref[h, rows, :] + jnp.sum(p, axis=1, keepdims=True)
            m_ref[h, rows, :] = m_next
            pv = jnp.dot(p.astype(v.dtype), v, preferred_element_type=jnp.float32)
            alphas.append(alpha)
            pvs.append(pv)
        alpha_b = jnp.where(lane, alphas[0], alphas[1])
        pv_b = jnp.where(lane, pvs[0], pvs[1])
        acc_ref[rows, :] = alpha_b * acc_ref[rows, :] + pv_b

    @pl.when(active)
    def _():
        for r in range(rows_all // ROW_BLOCK):
            qk_off = scal_ref[0] if r < half_blocks else scal_ref[1]
            dmin = qk_off + r * ROW_BLOCK - (t * tk + tk - 1)
            dmax = qk_off + r * ROW_BLOCK + ROW_BLOCK - 1 - t * tk

            @pl.when(dmin >= far_edge)
            def _():
                update(r, False, qk_off)

            @pl.when((dmin < far_edge) & (dmax >= 0))
            def _():
                update(r, True, qk_off)


def attend(state, q, keys, values, offsets, n_valid, skip, dtab):
    m, l, acc = state
    rows, width = q.shape
    n_tiles = keys.shape[0] // KEY_TILE
    scal = jnp.stack(
        [jnp.asarray(x, jnp.int32) for x in (offsets[0], offsets[1], n_valid, skip[0], skip[1])]
    )

    def tile_map(t, sc):
        return (jnp.maximum(jnp.minimum(t, sc[2] - 1), 0), 0)

    full2 = lambda t, sc: (0, 0)
    full3 = lambda t, sc: (0, 0, 0)
    flops = 8 * rows * KEY_TILE * width * n_tiles * 2
    cost = pl.CostEstimate(
        flops=flops,
        transcendentals=2 * rows * KEY_TILE * n_tiles,
        bytes_accessed=2 * keys.size * 2 + 6 * rows * width * 4,
    )
    return pl.pallas_call(
        attn_kernel,
        out_shape=(
            jax.ShapeDtypeStruct(m.shape, jnp.float32),
            jax.ShapeDtypeStruct(l.shape, jnp.float32),
            jax.ShapeDtypeStruct(acc.shape, jnp.float32),
        ),
        grid_spec=pltpu.PrefetchScalarGridSpec(
            num_scalar_prefetch=1,
            grid=(n_tiles,),
            in_specs=[
                pl.BlockSpec(memory_space=pltpu.SMEM),
                pl.BlockSpec((rows, width), full2),
                pl.BlockSpec((KEY_TILE, width), tile_map),
                pl.BlockSpec((KEY_TILE, width), tile_map),
                pl.BlockSpec(m.shape, full3),
                pl.BlockSpec(l.shape, full3),
                pl.BlockSpec(acc.shape, full2),
            ],
            out_specs=[
                pl.BlockSpec(m.shape, full3),
                pl.BlockSpec(l.shape, full3),
                pl.BlockSpec(acc.shape, full2),
            ],
        ),
        compiler_params=pltpu.CompilerParams(dimension_semantics=("arbitrary",)),
        cost_estimate=cost,
    )(scal, dtab, q, keys, values, m, l, acc)


def rms_scale(rows, gain):
    return (
        rows * lax.rsqrt(jnp.mean(rows * rows, axis=-1, keepdims=True) + epsilon) * gain
    ).astype(jnp.bfloat16)


def per_device(
    layer_input,
    queries,
    fresh_keys,
    fresh_values,
    cached_keys,
    cached_values,
    start_position,
    bias_table,
    out_weight,
    norm_gain,
    routes,
    route_weights,
    expert_in,
    expert_out,
):
    tok_rows = queries.shape[0]
    width = queries.shape[1]
    half = tok_rows // 2
    offset = start_position[0]
    n_seq = lax.axis_size("seq")
    seq_index = lax.axis_index("seq")
    partner = n_seq - 1 - seq_index
    swap = [(i, n_seq - 1 - i) for i in range(n_seq)]
    rows_q = jnp.concatenate([queries[:half], lax.ppermute(queries[half:], "seq", swap)], 0)
    dtab = bias_table - bias_table[bias_table.shape[0] - 1][None, :]
    state = (
        jnp.full((2, tok_rows, 128), lowest, jnp.float32),
        jnp.zeros((2, tok_rows, 128), jnp.float32),
        jnp.zeros((tok_rows, width), jnp.float32),
    )
    own_tiles = fresh_keys.shape[0] // KEY_TILE
    no_skip = (0, 0)
    state = attend(
        state,
        rows_q,
        fresh_keys,
        fresh_values,
        (0, (partner - seq_index) * tok_rows),
        own_tiles,
        no_skip,
        dtab,
    )
    prior_k = lax.all_gather(cached_keys, "seq", axis=0, tiled=True)
    prior_v = lax.all_gather(cached_values, "seq", axis=0, tiled=True)
    state = attend(
        state,
        rows_q,
        prior_k,
        prior_v,
        (offset + seq_index * tok_rows, offset + partner * tok_rows),
        prior_k.shape[0] // KEY_TILE,
        no_skip,
        dtab,
    )
    all_k = lax.all_gather(fresh_keys, "seq", axis=0, tiled=True)
    all_v = lax.all_gather(fresh_values, "seq", axis=0, tiled=True)
    state = attend(
        state,
        rows_q,
        all_k,
        all_v,
        (seq_index * tok_rows, partner * tok_rows),
        jnp.maximum(seq_index * own_tiles + own_tiles // 2, (partner + 1) * own_tiles),
        (seq_index * own_tiles, (seq_index + 1) * own_tiles),
        dtab,
    )
    m, l, acc = state
    lane = lax.broadcasted_iota(jnp.int32, (1, width), 1) < HEAD_DIM
    totals = jnp.where(lane, l[0], l[1])
    done_rows = (acc / totals).astype(jnp.bfloat16)
    attended = jnp.concatenate([done_rows[:half], lax.ppermute(done_rows[half:], "seq", swap)], 0)
    attended_full = lax.all_gather(attended, "tensor", axis=1, tiled=True)
    weight_full = lax.all_gather(out_weight, "tensor", axis=0, tiled=True)
    col_width = D // lax.axis_size("tensor")
    col_start = lax.axis_index("tensor") * col_width
    resid = layer_input.astype(jnp.float32) + jnp.dot(
        attended_full, weight_full, preferred_element_type=jnp.float32
    )
    normed = rms_scale(resid, norm_gain)
    resid_cols = lax.dynamic_slice_in_dim(resid, col_start, col_width, 1)
    expert_count = expert_in.shape[0]
    flat_routes = routes.reshape(-1)
    onehot = (flat_routes[:, None] == jnp.arange(expert_count, dtype=jnp.int32)[None, :]).astype(
        jnp.int32
    )
    before = jnp.cumsum(onehot, axis=0) - onehot
    slot = jnp.sum(before * onehot, axis=1)
    target = flat_routes * CAP + slot
    owner = jnp.arange(flat_routes.shape[0], dtype=jnp.int32) // TOP
    slot_owner = jnp.zeros((expert_count * CAP,), jnp.int32).at[target].set(owner)
    buffer = jnp.take(normed, slot_owner, axis=0).reshape(expert_count, CAP, D)
    gate_up = jnp.einsum("ecd,edgf->ecgf", buffer, expert_in, preferred_element_type=jnp.float32)
    hidden = (jax.nn.gelu(gate_up[:, :, 0], approximate=True) * gate_up[:, :, 1]).astype(
        jnp.bfloat16
    )
    expert_rows = jnp.einsum(
        "ecf,efd->ecd", hidden, expert_out, preferred_element_type=jnp.float32
    ).reshape(expert_count * CAP, D)
    picked = jnp.take(expert_rows, target, axis=0).reshape(tok_rows, TOP, D)
    combined = jnp.sum(picked * route_weights[:, :, None], axis=1)
    expert_cols = lax.psum_scatter(
        combined.astype(jnp.bfloat16), "tensor", scatter_dimension=1, tiled=True
    ).astype(jnp.float32)
    return (resid_cols + expert_cols).astype(jnp.bfloat16)


def solution(mesh):
    return jax.shard_map(
        per_device,
        mesh=mesh,
        in_specs=(
            P("seq", None),
            P("seq", "tensor"),
            P("seq", "tensor"),
            P("seq", "tensor"),
            P("seq", "tensor"),
            P("seq", "tensor"),
            P(),
            P(None, "tensor"),
            P("tensor", None),
            P(),
            P("seq", None),
            P("seq", None),
            P(None, None, None, "tensor"),
            P(None, "tensor", None),
        ),
        out_specs=P("seq", "tensor"),
        check_vma=False,
    )
```

```python
import math

import jax
import jax.numpy as jnp
from jax import lax
from jax.experimental import pallas as pl
from jax.experimental.pallas import tpu as pltpu
from jax.sharding import PartitionSpec as P

D = 1024
HEAD_DIM = 64
TOP = 2
CAP = 384
KEY_TILE = 512
ROW_BLOCK = 128


bucket_edges = [edge for edge in range(1, 17)] + [
    math.ceil(16 * 8 ** (level / 16)) for level in range(1, 16)
]
far_edge = bucket_edges[-1]
epsilon = 1e-06
lowest = -1e30


def attn_kernel(scal_ref, dtab_ref, q_ref, k_ref, v_ref, m_in, l_in, acc_in, m_ref, l_ref, acc_ref):
    t = pl.program_id(0)
    tk = k_ref.shape[0]
    rows_all = q_ref.shape[0]

    @pl.when(t == 0)
    def _():
        m_ref[...] = m_in[...]
        l_ref[...] = l_in[...]
        acc_ref[...] = acc_in[...]

    n_valid = scal_ref[2]
    stride = scal_ref[5]
    active = (t < n_valid) & ((t < scal_ref[3]) | (t >= scal_ref[4]))
    half_blocks = rows_all // ROW_BLOCK // 2

    def update(r, near, qk_off):
        rows = pl.ds(r * ROW_BLOCK, ROW_BLOCK)
        q = q_ref[rows, :]
        k = k_ref[...]
        v = v_ref[...]
        lane = lax.broadcasted_iota(jnp.int32, (1, q.shape[1]), 1) < HEAD_DIM
        zero_q = jnp.zeros_like(q)
        if near:
            base = qk_off + r * ROW_BLOCK - t * stride
            d = (
                base
                + lax.broadcasted_iota(jnp.int32, (ROW_BLOCK, tk), 0)
                - lax.broadcasted_iota(jnp.int32, (ROW_BLOCK, tk), 1)
            )
            allowed = d >= 0
            bucket = jnp.zeros(d.shape, jnp.int32)
            for edge in bucket_edges:
                bucket = bucket + (d >= edge).astype(jnp.int32)
        news = []
        alphas = []
        pvs = []
        for h in range(2):
            qh = jnp.where(lane, q, zero_q) if h == 0 else jnp.where(lane, zero_q, q)
            s = lax.dot_general(
                qh, k, (((1,), (1,)), ((), ())), preferred_element_type=jnp.float32
            )
            if near:
                delta = jnp.zeros(s.shape, jnp.float32)
                for level in range(len(bucket_edges)):
                    delta = jnp.where(bucket == level, dtab_ref[level, h], delta)
                s = jnp.where(allowed, s + delta, -jnp.inf)
            m_prev = m_ref[h, rows, :]
            m_curr = jnp.max(s, axis=1, keepdims=True)
            m_next = jnp.maximum(m_prev, m_curr)
            p = jnp.exp(s - jnp.tile(m_next, (1, tk // m_next.shape[1])))
            alpha = jnp.exp(m_prev - m_next)
            l_ref[h, rows, :] = alpha * l_ref[h, rows, :] + jnp.sum(p, axis=1, keepdims=True)
            m_ref[h, rows, :] = m_next
            pv = jnp.dot(p.astype(v.dtype), v, preferred_element_type=jnp.float32)
            alphas.append(alpha)
            pvs.append(pv)
        alpha_b = jnp.where(lane, alphas[0], alphas[1])
        pv_b = jnp.where(lane, pvs[0], pvs[1])
        acc_ref[rows, :] = alpha_b * acc_ref[rows, :] + pv_b

    @pl.when(active)
    def _():
        for r in range(rows_all // ROW_BLOCK):
            qk_off = scal_ref[0] if r < half_blocks else scal_ref[1]
            dmin = qk_off + r * ROW_BLOCK - (t * stride + tk - 1)
            dmax = qk_off + r * ROW_BLOCK + ROW_BLOCK - 1 - t * stride

            @pl.when(dmin >= far_edge)
            def _():
                update(r, False, qk_off)

            @pl.when((dmin < far_edge) & (dmax >= 0))
            def _():
                update(r, True, qk_off)


def attend(state, q, keys, values, offsets, n_valid, skip, dtab, stride=KEY_TILE):
    m, l, acc = state
    rows, width = q.shape
    n_tiles = keys.shape[0] // KEY_TILE
    scal = jnp.stack(
        [
            jnp.asarray(x, jnp.int32)
            for x in (offsets[0], offsets[1], n_valid, skip[0], skip[1], stride)
        ]
    )

    def tile_map(t, sc):
        return (jnp.maximum(jnp.minimum(t, sc[2] - 1), 0), 0)

    full2 = lambda t, sc: (0, 0)
    full3 = lambda t, sc: (0, 0, 0)
    flops = 8 * rows * KEY_TILE * width * n_tiles * 2
    cost = pl.CostEstimate(
        flops=flops,
        transcendentals=2 * rows * KEY_TILE * n_tiles,
        bytes_accessed=2 * keys.size * 2 + 6 * rows * width * 4,
    )
    return pl.pallas_call(
        attn_kernel,
        out_shape=(
            jax.ShapeDtypeStruct(m.shape, jnp.float32),
            jax.ShapeDtypeStruct(l.shape, jnp.float32),
            jax.ShapeDtypeStruct(acc.shape, jnp.float32),
        ),
        grid_spec=pltpu.PrefetchScalarGridSpec(
            num_scalar_prefetch=1,
            grid=(n_tiles,),
            in_specs=[
                pl.BlockSpec(memory_space=pltpu.SMEM),
                pl.BlockSpec((rows, width), full2),
                pl.BlockSpec((KEY_TILE, width), tile_map),
                pl.BlockSpec((KEY_TILE, width), tile_map),
                pl.BlockSpec(m.shape, full3),
                pl.BlockSpec(l.shape, full3),
                pl.BlockSpec(acc.shape, full2),
            ],
            out_specs=[
                pl.BlockSpec(m.shape, full3),
                pl.BlockSpec(l.shape, full3),
                pl.BlockSpec(acc.shape, full2),
            ],
        ),
        compiler_params=pltpu.CompilerParams(dimension_semantics=("arbitrary",)),
        cost_estimate=cost,
    )(scal, dtab, q, keys, values, m, l, acc)


def rms_scale(rows, gain):
    return (
        rows * lax.rsqrt(jnp.mean(rows * rows, axis=-1, keepdims=True) + epsilon) * gain
    ).astype(jnp.bfloat16)


def per_device(
    layer_input,
    queries,
    fresh_keys,
    fresh_values,
    cached_keys,
    cached_values,
    start_position,
    bias_table,
    out_weight,
    norm_gain,
    routes,
    route_weights,
    expert_in,
    expert_out,
):
    tok_rows = queries.shape[0]
    width = queries.shape[1]
    half = tok_rows // 2
    offset = start_position[0]
    n_seq = lax.axis_size("seq")
    seq_index = lax.axis_index("seq")
    partner = n_seq - 1 - seq_index
    swap = [(i, n_seq - 1 - i) for i in range(n_seq)]
    rows_q = jnp.concatenate([queries[:half], lax.ppermute(queries[half:], "seq", swap)], 0)
    dtab = bias_table - bias_table[bias_table.shape[0] - 1][None, :]
    state = (
        jnp.full((2, tok_rows, 128), lowest, jnp.float32),
        jnp.zeros((2, tok_rows, 128), jnp.float32),
        jnp.zeros((tok_rows, width), jnp.float32),
    )
    own_tiles = fresh_keys.shape[0] // KEY_TILE
    no_skip = (0, 0)
    state = attend(
        state,
        rows_q,
        fresh_keys,
        fresh_values,
        (0, (partner - seq_index) * tok_rows),
        own_tiles,
        no_skip,
        dtab,
    )
    prior_rows = cached_keys.shape[0]
    split = prior_rows - KEY_TILE
    for lo, hi in ((0, split), (split, prior_rows)):
        prior_k = lax.all_gather(cached_keys[lo:hi], "seq", axis=0, tiled=True)
        prior_v = lax.all_gather(cached_values[lo:hi], "seq", axis=0, tiled=True)
        state = attend(
            state,
            rows_q,
            prior_k,
            prior_v,
            (offset + seq_index * tok_rows - lo, offset + partner * tok_rows - lo),
            prior_k.shape[0] // KEY_TILE,
            no_skip,
            dtab,
            KEY_TILE if lo == 0 else prior_rows,
        )
    all_k = lax.all_gather(fresh_keys, "seq", axis=0, tiled=True)
    all_v = lax.all_gather(fresh_values, "seq", axis=0, tiled=True)
    state = attend(
        state,
        rows_q,
        all_k,
        all_v,
        (seq_index * tok_rows, partner * tok_rows),
        jnp.maximum(seq_index * own_tiles + own_tiles // 2, (partner + 1) * own_tiles),
        (seq_index * own_tiles, (seq_index + 1) * own_tiles),
        dtab,
    )
    m, l, acc = state
    lane = lax.broadcasted_iota(jnp.int32, (1, width), 1) < HEAD_DIM
    totals = jnp.where(lane, l[0], l[1])
    done_rows = (acc / totals).astype(jnp.bfloat16)
    attended = jnp.concatenate([done_rows[:half], lax.ppermute(done_rows[half:], "seq", swap)], 0)
    attended_full = lax.all_gather(attended, "tensor", axis=1, tiled=True)
    weight_full = lax.all_gather(out_weight, "tensor", axis=0, tiled=True)
    col_width = D // lax.axis_size("tensor")
    col_start = lax.axis_index("tensor") * col_width
    resid = layer_input.astype(jnp.float32) + jnp.dot(
        attended_full, weight_full, preferred_element_type=jnp.float32
    )
    normed = rms_scale(resid, norm_gain)
    resid_cols = lax.dynamic_slice_in_dim(resid, col_start, col_width, 1)
    expert_count = expert_in.shape[0]
    flat_routes = routes.reshape(-1)
    onehot = (flat_routes[:, None] == jnp.arange(expert_count, dtype=jnp.int32)[None, :]).astype(
        jnp.int32
    )
    before = jnp.cumsum(onehot, axis=0) - onehot
    slot = jnp.sum(before * onehot, axis=1)
    target = flat_routes * CAP + slot
    owner = jnp.arange(flat_routes.shape[0], dtype=jnp.int32) // TOP
    slot_owner = jnp.zeros((expert_count * CAP,), jnp.int32).at[target].set(owner)
    buffer = jnp.take(normed, slot_owner, axis=0).reshape(expert_count, CAP, D)
    gate_up = jnp.einsum("ecd,edgf->ecgf", buffer, expert_in, preferred_element_type=jnp.float32)
    hidden = (jax.nn.gelu(gate_up[:, :, 0], approximate=True) * gate_up[:, :, 1]).astype(
        jnp.bfloat16
    )
    expert_rows = jnp.einsum(
        "ecf,efd->ecd", hidden, expert_out, preferred_element_type=jnp.float32
    ).reshape(expert_count * CAP, D)
    picked = jnp.take(expert_rows, target, axis=0).reshape(tok_rows, TOP, D)
    combined = jnp.sum(picked * route_weights[:, :, None], axis=1)
    expert_cols = lax.psum_scatter(
        combined.astype(jnp.bfloat16), "tensor", scatter_dimension=1, tiled=True
    ).astype(jnp.float32)
    return (resid_cols + expert_cols).astype(jnp.bfloat16)


def solution(mesh):
    return jax.shard_map(
        per_device,
        mesh=mesh,
        in_specs=(
            P("seq", None),
            P("seq", "tensor"),
            P("seq", "tensor"),
            P("seq", "tensor"),
            P("seq", "tensor"),
            P("seq", "tensor"),
            P(),
            P(None, "tensor"),
            P("tensor", None),
            P(),
            P("seq", None),
            P("seq", None),
            P(None, None, None, "tensor"),
            P(None, "tensor", None),
        ),
        out_specs=P("seq", "tensor"),
        check_vma=False,
    )
```

```python
import math

import jax
import jax.numpy as jnp
from jax import lax
from jax.experimental import pallas as pl
from jax.experimental.pallas import tpu as pltpu
from jax.sharding import PartitionSpec as P

D = 1024
HEAD_DIM = 64
TOP = 2
CAP = 384
KEY_TILE = 512
ROW_BLOCK = 128


bucket_edges = [edge for edge in range(1, 17)] + [
    math.ceil(16 * 8 ** (level / 16)) for level in range(1, 16)
]
far_edge = bucket_edges[-1]
epsilon = 1e-06
lowest = -1e30


def attn_kernel(scal_ref, dtab_ref, q_ref, k_ref, v_ref, m_in, l_in, acc_in, m_ref, l_ref, acc_ref):
    t = pl.program_id(0)
    tk = k_ref.shape[0]
    rows_all = q_ref.shape[0]

    @pl.when(t == 0)
    def _():
        m_ref[...] = m_in[...]
        l_ref[...] = l_in[...]
        acc_ref[...] = acc_in[...]

    n_valid = scal_ref[2]
    active = (t < n_valid) & ((t < scal_ref[3]) | (t >= scal_ref[4]))
    half_blocks = rows_all // ROW_BLOCK // 2

    def update(r, near, qk_off):
        rows = pl.ds(r * ROW_BLOCK, ROW_BLOCK)
        q = q_ref[rows, :]
        k = k_ref[...]
        v = v_ref[...]
        lane = lax.broadcasted_iota(jnp.int32, (1, q.shape[1]), 1) < HEAD_DIM
        zero_q = jnp.zeros_like(q)
        if near:
            base = qk_off + r * ROW_BLOCK - t * tk
            d = (
                base
                + lax.broadcasted_iota(jnp.int32, (ROW_BLOCK, tk), 0)
                - lax.broadcasted_iota(jnp.int32, (ROW_BLOCK, tk), 1)
            )
            allowed = d >= 0
            bucket = jnp.zeros(d.shape, jnp.int32)
            for edge in bucket_edges:
                bucket = bucket + (d >= edge).astype(jnp.int32)
        news = []
        alphas = []
        pvs = []
        for h in range(2):
            qh = jnp.where(lane, q, zero_q) if h == 0 else jnp.where(lane, zero_q, q)
            s = lax.dot_general(
                qh, k, (((1,), (1,)), ((), ())), preferred_element_type=jnp.float32
            )
            if near:
                delta = jnp.zeros(s.shape, jnp.float32)
                for level in range(len(bucket_edges)):
                    delta = jnp.where(bucket == level, dtab_ref[level, h], delta)
                s = jnp.where(allowed, s + delta, -jnp.inf)
            m_prev = m_ref[h, rows, :]
            m_curr = jnp.max(s, axis=1, keepdims=True)
            m_next = jnp.maximum(m_prev, m_curr)
            p = jnp.exp(s - jnp.tile(m_next, (1, tk // m_next.shape[1])))
            alpha = jnp.exp(m_prev - m_next)
            l_ref[h, rows, :] = alpha * l_ref[h, rows, :] + jnp.sum(p, axis=1, keepdims=True)
            m_ref[h, rows, :] = m_next
            pv = jnp.dot(p.astype(v.dtype), v, preferred_element_type=jnp.float32)
            alphas.append(alpha)
            pvs.append(pv)
        alpha_b = jnp.where(lane, alphas[0], alphas[1])
        pv_b = jnp.where(lane, pvs[0], pvs[1])
        acc_ref[rows, :] = alpha_b * acc_ref[rows, :] + pv_b

    @pl.when(active)
    def _():
        for r in range(rows_all // ROW_BLOCK):
            qk_off = scal_ref[0] if r < half_blocks else scal_ref[1]
            dmin = qk_off + r * ROW_BLOCK - (t * tk + tk - 1)
            dmax = qk_off + r * ROW_BLOCK + ROW_BLOCK - 1 - t * tk

            @pl.when(dmin >= far_edge)
            def _():
                update(r, False, qk_off)

            @pl.when((dmin < far_edge) & (dmax >= 0))
            def _():
                update(r, True, qk_off)


def attend(state, q, pairs, offsets, n_valid, skip, dtab):
    m, l, acc = state
    rows, width = q.shape
    n_tiles = pairs.shape[0] // KEY_TILE
    scal = jnp.stack(
        [jnp.asarray(x, jnp.int32) for x in (offsets[0], offsets[1], n_valid, skip[0], skip[1])]
    )

    def tile_index(t, sc):
        return jnp.maximum(jnp.minimum(t, sc[2] - 1), 0)

    key_map = lambda t, sc: (tile_index(t, sc), 0)
    value_map = lambda t, sc: (tile_index(t, sc), 1)

    full2 = lambda t, sc: (0, 0)
    full3 = lambda t, sc: (0, 0, 0)
    flops = 8 * rows * KEY_TILE * width * n_tiles * 2
    cost = pl.CostEstimate(
        flops=flops,
        transcendentals=2 * rows * KEY_TILE * n_tiles,
        bytes_accessed=pairs.size * 2 + 6 * rows * width * 4,
    )
    return pl.pallas_call(
        attn_kernel,
        out_shape=(
            jax.ShapeDtypeStruct(m.shape, jnp.float32),
            jax.ShapeDtypeStruct(l.shape, jnp.float32),
            jax.ShapeDtypeStruct(acc.shape, jnp.float32),
        ),
        grid_spec=pltpu.PrefetchScalarGridSpec(
            num_scalar_prefetch=1,
            grid=(n_tiles,),
            in_specs=[
                pl.BlockSpec(memory_space=pltpu.SMEM),
                pl.BlockSpec((rows, width), full2),
                pl.BlockSpec((KEY_TILE, width), key_map),
                pl.BlockSpec((KEY_TILE, width), value_map),
                pl.BlockSpec(m.shape, full3),
                pl.BlockSpec(l.shape, full3),
                pl.BlockSpec(acc.shape, full2),
            ],
            out_specs=[
                pl.BlockSpec(m.shape, full3),
                pl.BlockSpec(l.shape, full3),
                pl.BlockSpec(acc.shape, full2),
            ],
        ),
        compiler_params=pltpu.CompilerParams(dimension_semantics=("arbitrary",)),
        cost_estimate=cost,
    )(scal, dtab, q, pairs, pairs, m, l, acc)


def rms_scale(rows, gain):
    return (
        rows * lax.rsqrt(jnp.mean(rows * rows, axis=-1, keepdims=True) + epsilon) * gain
    ).astype(jnp.bfloat16)


def per_device(
    layer_input,
    queries,
    fresh_keys,
    fresh_values,
    cached_keys,
    cached_values,
    start_position,
    bias_table,
    out_weight,
    norm_gain,
    routes,
    route_weights,
    expert_in,
    expert_out,
):
    tok_rows = queries.shape[0]
    width = queries.shape[1]
    half = tok_rows // 2
    offset = start_position[0]
    n_seq = lax.axis_size("seq")
    seq_index = lax.axis_index("seq")
    partner = n_seq - 1 - seq_index
    swap = [(i, n_seq - 1 - i) for i in range(n_seq)]
    rows_q = jnp.concatenate([queries[:half], lax.ppermute(queries[half:], "seq", swap)], 0)
    dtab = bias_table - bias_table[bias_table.shape[0] - 1][None, :]
    state = (
        jnp.full((2, tok_rows, 128), lowest, jnp.float32),
        jnp.zeros((2, tok_rows, 128), jnp.float32),
        jnp.zeros((tok_rows, width), jnp.float32),
    )
    own_tiles = fresh_keys.shape[0] // KEY_TILE
    no_skip = (0, 0)
    own_pairs = jnp.concatenate([fresh_keys, fresh_values], 1)
    state = attend(
        state,
        rows_q,
        own_pairs,
        (0, (partner - seq_index) * tok_rows),
        own_tiles,
        no_skip,
        dtab,
    )
    prior_pairs = lax.all_gather(
        jnp.concatenate([cached_keys, cached_values], 1), "seq", axis=0, tiled=True
    )
    state = attend(
        state,
        rows_q,
        prior_pairs,
        (offset + seq_index * tok_rows, offset + partner * tok_rows),
        prior_pairs.shape[0] // KEY_TILE,
        no_skip,
        dtab,
    )
    all_pairs = lax.all_gather(own_pairs, "seq", axis=0, tiled=True)
    state = attend(
        state,
        rows_q,
        all_pairs,
        (seq_index * tok_rows, partner * tok_rows),
        jnp.maximum(seq_index * own_tiles + own_tiles // 2, (partner + 1) * own_tiles),
        (seq_index * own_tiles, (seq_index + 1) * own_tiles),
        dtab,
    )
    m, l, acc = state
    lane = lax.broadcasted_iota(jnp.int32, (1, width), 1) < HEAD_DIM
    totals = jnp.where(lane, l[0], l[1])
    done_rows = (acc / totals).astype(jnp.bfloat16)
    attended = jnp.concatenate([done_rows[:half], lax.ppermute(done_rows[half:], "seq", swap)], 0)
    attended_full = lax.all_gather(attended, "tensor", axis=1, tiled=True)
    weight_full = lax.all_gather(out_weight, "tensor", axis=0, tiled=True)
    col_width = D // lax.axis_size("tensor")
    col_start = lax.axis_index("tensor") * col_width
    resid = layer_input.astype(jnp.float32) + jnp.dot(
        attended_full, weight_full, preferred_element_type=jnp.float32
    )
    normed = rms_scale(resid, norm_gain)
    resid_cols = lax.dynamic_slice_in_dim(resid, col_start, col_width, 1)
    expert_count = expert_in.shape[0]
    flat_routes = routes.reshape(-1)
    onehot = (flat_routes[:, None] == jnp.arange(expert_count, dtype=jnp.int32)[None, :]).astype(
        jnp.int32
    )
    before = jnp.cumsum(onehot, axis=0) - onehot
    slot = jnp.sum(before * onehot, axis=1)
    target = flat_routes * CAP + slot
    owner = jnp.arange(flat_routes.shape[0], dtype=jnp.int32) // TOP
    slot_owner = jnp.zeros((expert_count * CAP,), jnp.int32).at[target].set(owner)
    buffer = jnp.take(normed, slot_owner, axis=0).reshape(expert_count, CAP, D)
    gate_up = jnp.einsum("ecd,edgf->ecgf", buffer, expert_in, preferred_element_type=jnp.float32)
    hidden = (jax.nn.gelu(gate_up[:, :, 0], approximate=True) * gate_up[:, :, 1]).astype(
        jnp.bfloat16
    )
    expert_rows = jnp.einsum(
        "ecf,efd->ecd", hidden, expert_out, preferred_element_type=jnp.float32
    ).reshape(expert_count * CAP, D)
    picked = jnp.take(expert_rows, target, axis=0).reshape(tok_rows, TOP, D)
    combined = jnp.sum(picked * route_weights[:, :, None], axis=1)
    expert_cols = lax.psum_scatter(
        combined.astype(jnp.bfloat16), "tensor", scatter_dimension=1, tiled=True
    ).astype(jnp.float32)
    return (resid_cols + expert_cols).astype(jnp.bfloat16)


def solution(mesh):
    return jax.shard_map(
        per_device,
        mesh=mesh,
        in_specs=(
            P("seq", None),
            P("seq", "tensor"),
            P("seq", "tensor"),
            P("seq", "tensor"),
            P("seq", "tensor"),
            P("seq", "tensor"),
            P(),
            P(None, "tensor"),
            P("tensor", None),
            P(),
            P("seq", None),
            P("seq", None),
            P(None, None, None, "tensor"),
            P(None, "tensor", None),
        ),
        out_specs=P("seq", "tensor"),
        check_vma=False,
    )
```

```python
import math

import jax
import jax.numpy as jnp
from jax import lax
from jax.experimental import pallas as pl
from jax.experimental.pallas import tpu as pltpu
from jax.sharding import PartitionSpec as P

D = 1024
HEAD_DIM = 64
TOP = 2
CAP = 384
KEY_TILE = 512
ROW_BLOCK = 128


bucket_edges = [edge for edge in range(1, 17)] + [
    math.ceil(16 * 8 ** (level / 16)) for level in range(1, 16)
]
far_edge = bucket_edges[-1]
epsilon = 1e-06
lowest = -1e30


def attn_kernel(scal_ref, dtab_ref, q_ref, k_ref, v_ref, m_in, l_in, acc_in, m_ref, l_ref, acc_ref):
    t = pl.program_id(0)
    tk = k_ref.shape[0]
    rows_all = q_ref.shape[0]

    @pl.when(t == 0)
    def _():
        m_ref[...] = m_in[...]
        l_ref[...] = l_in[...]
        acc_ref[...] = acc_in[...]

    n_valid = scal_ref[2]
    active = (t < n_valid) & ((t < scal_ref[3]) | (t >= scal_ref[4]))
    half_blocks = rows_all // ROW_BLOCK // 2

    def update(r, near, qk_off):
        rows = pl.ds(r * ROW_BLOCK, ROW_BLOCK)
        q = q_ref[rows, :]
        k = k_ref[...]
        v = v_ref[...]
        lane = lax.broadcasted_iota(jnp.int32, (1, q.shape[1]), 1) < HEAD_DIM
        zero_q = jnp.zeros_like(q)
        if near:
            base = qk_off + r * ROW_BLOCK - t * tk
            d = (
                base
                + lax.broadcasted_iota(jnp.int32, (ROW_BLOCK, tk), 0)
                - lax.broadcasted_iota(jnp.int32, (ROW_BLOCK, tk), 1)
            )
            allowed = d >= 0
            bucket = jnp.zeros(d.shape, jnp.int32)
            for edge in bucket_edges:
                bucket = bucket + (d >= edge).astype(jnp.int32)
        news = []
        alphas = []
        pvs = []
        for h in range(2):
            qh = jnp.where(lane, q, zero_q) if h == 0 else jnp.where(lane, zero_q, q)
            s = lax.dot_general(
                qh, k, (((1,), (1,)), ((), ())), preferred_element_type=jnp.float32
            )
            if near:
                delta = jnp.zeros(s.shape, jnp.float32)
                for level in range(len(bucket_edges)):
                    delta = jnp.where(bucket == level, dtab_ref[level, h], delta)
                s = jnp.where(allowed, s + delta, -jnp.inf)
            m_prev = m_ref[h, rows, :]
            m_curr = jnp.max(s, axis=1, keepdims=True)
            m_next = jnp.maximum(m_prev, m_curr)
            p = jnp.exp(s - jnp.tile(m_next, (1, tk // m_next.shape[1])))
            alpha = jnp.exp(m_prev - m_next)
            l_ref[h, rows, :] = alpha * l_ref[h, rows, :] + jnp.sum(p, axis=1, keepdims=True)
            m_ref[h, rows, :] = m_next
            pv = jnp.dot(p.astype(v.dtype), v, preferred_element_type=jnp.float32)
            alphas.append(alpha)
            pvs.append(pv)
        alpha_b = jnp.where(lane, alphas[0], alphas[1])
        pv_b = jnp.where(lane, pvs[0], pvs[1])
        acc_ref[rows, :] = alpha_b * acc_ref[rows, :] + pv_b

    @pl.when(active)
    def _():
        for r in range(rows_all // ROW_BLOCK):
            qk_off = scal_ref[0] if r < half_blocks else scal_ref[1]
            dmin = qk_off + r * ROW_BLOCK - (t * tk + tk - 1)
            dmax = qk_off + r * ROW_BLOCK + ROW_BLOCK - 1 - t * tk

            @pl.when(dmin >= far_edge)
            def _():
                update(r, False, qk_off)

            @pl.when((dmin < far_edge) & (dmax >= 0))
            def _():
                update(r, True, qk_off)


def attend(state, q, pairs, offsets, n_valid, skip, dtab):
    m, l, acc = state
    rows, width = q.shape
    n_tiles = pairs.shape[0] // KEY_TILE
    scal = jnp.stack(
        [jnp.asarray(x, jnp.int32) for x in (offsets[0], offsets[1], n_valid, skip[0], skip[1])]
    )

    def tile_index(t, sc):
        return jnp.maximum(jnp.minimum(t, sc[2] - 1), 0)

    key_map = lambda t, sc: (tile_index(t, sc), 0)
    value_map = lambda t, sc: (tile_index(t, sc), 1)

    full2 = lambda t, sc: (0, 0)
    full3 = lambda t, sc: (0, 0, 0)
    flops = 8 * rows * KEY_TILE * width * n_tiles * 2
    cost = pl.CostEstimate(
        flops=flops,
        transcendentals=2 * rows * KEY_TILE * n_tiles,
        bytes_accessed=pairs.size * 2 + 6 * rows * width * 4,
    )
    return pl.pallas_call(
        attn_kernel,
        out_shape=(
            jax.ShapeDtypeStruct(m.shape, jnp.float32),
            jax.ShapeDtypeStruct(l.shape, jnp.float32),
            jax.ShapeDtypeStruct(acc.shape, jnp.float32),
        ),
        grid_spec=pltpu.PrefetchScalarGridSpec(
            num_scalar_prefetch=1,
            grid=(n_tiles,),
            in_specs=[
                pl.BlockSpec(memory_space=pltpu.SMEM),
                pl.BlockSpec((rows, width), full2),
                pl.BlockSpec((KEY_TILE, width), key_map),
                pl.BlockSpec((KEY_TILE, width), value_map),
                pl.BlockSpec(m.shape, full3),
                pl.BlockSpec(l.shape, full3),
                pl.BlockSpec(acc.shape, full2),
            ],
            out_specs=[
                pl.BlockSpec(m.shape, full3),
                pl.BlockSpec(l.shape, full3),
                pl.BlockSpec(acc.shape, full2),
            ],
        ),
        compiler_params=pltpu.CompilerParams(dimension_semantics=("arbitrary",)),
        cost_estimate=cost,
    )(scal, dtab, q, pairs, pairs, m, l, acc)


def rms_scale(rows, gain):
    return (
        rows * lax.rsqrt(jnp.mean(rows * rows, axis=-1, keepdims=True) + epsilon) * gain
    ).astype(jnp.bfloat16)


def per_device(
    layer_input,
    queries,
    fresh_keys,
    fresh_values,
    cached_keys,
    cached_values,
    start_position,
    bias_table,
    out_weight,
    norm_gain,
    routes,
    route_weights,
    expert_in,
    expert_out,
):
    tok_rows = queries.shape[0]
    width = queries.shape[1]
    half = tok_rows // 2
    offset = start_position[0]
    n_seq = lax.axis_size("seq")
    seq_index = lax.axis_index("seq")
    partner = n_seq - 1 - seq_index
    swap = [(i, n_seq - 1 - i) for i in range(n_seq)]
    rows_q = jnp.concatenate([queries[:half], lax.ppermute(queries[half:], "seq", swap)], 0)
    expert_count = expert_in.shape[0]
    flat_routes = routes.reshape(-1)
    onehot = (flat_routes[:, None] == jnp.arange(expert_count, dtype=jnp.int32)[None, :]).astype(
        jnp.int32
    )
    before = jnp.cumsum(onehot, axis=0) - onehot
    slot = jnp.sum(before * onehot, axis=1)
    target = flat_routes * CAP + slot
    owner = jnp.arange(flat_routes.shape[0], dtype=jnp.int32) // TOP
    slot_owner = jnp.zeros((expert_count * CAP,), jnp.int32).at[target].set(owner)
    slot_owner, target, rows_q = lax.optimization_barrier((slot_owner, target, rows_q))
    dtab = bias_table - bias_table[bias_table.shape[0] - 1][None, :]
    state = (
        jnp.full((2, tok_rows, 128), lowest, jnp.float32),
        jnp.zeros((2, tok_rows, 128), jnp.float32),
        jnp.zeros((tok_rows, width), jnp.float32),
    )
    own_tiles = fresh_keys.shape[0] // KEY_TILE
    no_skip = (0, 0)
    own_pairs = jnp.concatenate([fresh_keys, fresh_values], 1)
    state = attend(
        state,
        rows_q,
        own_pairs,
        (0, (partner - seq_index) * tok_rows),
        own_tiles,
        no_skip,
        dtab,
    )
    prior_pairs = lax.all_gather(
        jnp.concatenate([cached_keys, cached_values], 1), "seq", axis=0, tiled=True
    )
    state = attend(
        state,
        rows_q,
        prior_pairs,
        (offset + seq_index * tok_rows, offset + partner * tok_rows),
        prior_pairs.shape[0] // KEY_TILE,
        no_skip,
        dtab,
    )
    all_pairs = lax.all_gather(own_pairs, "seq", axis=0, tiled=True)
    state = attend(
        state,
        rows_q,
        all_pairs,
        (seq_index * tok_rows, partner * tok_rows),
        jnp.maximum(seq_index * own_tiles + own_tiles // 2, (partner + 1) * own_tiles),
        (seq_index * own_tiles, (seq_index + 1) * own_tiles),
        dtab,
    )
    m, l, acc = state
    lane = lax.broadcasted_iota(jnp.int32, (1, width), 1) < HEAD_DIM
    totals = jnp.where(lane, l[0], l[1])
    done_rows = (acc / totals).astype(jnp.bfloat16)
    attended = jnp.concatenate([done_rows[:half], lax.ppermute(done_rows[half:], "seq", swap)], 0)
    attended_full = lax.all_gather(attended, "tensor", axis=1, tiled=True)
    weight_full = lax.all_gather(out_weight, "tensor", axis=0, tiled=True)
    col_width = D // lax.axis_size("tensor")
    col_start = lax.axis_index("tensor") * col_width
    resid = layer_input.astype(jnp.float32) + jnp.dot(
        attended_full, weight_full, preferred_element_type=jnp.float32
    )
    normed = rms_scale(resid, norm_gain)
    resid_cols = lax.dynamic_slice_in_dim(resid, col_start, col_width, 1)
    buffer = jnp.take(normed, slot_owner, axis=0).reshape(expert_count, CAP, D)
    gate_up = jnp.einsum("ecd,edgf->ecgf", buffer, expert_in, preferred_element_type=jnp.float32)
    hidden = (jax.nn.gelu(gate_up[:, :, 0], approximate=True) * gate_up[:, :, 1]).astype(
        jnp.bfloat16
    )
    expert_rows = jnp.einsum(
        "ecf,efd->ecd", hidden, expert_out, preferred_element_type=jnp.float32
    ).reshape(expert_count * CAP, D)
    picked = jnp.take(expert_rows, target, axis=0).reshape(tok_rows, TOP, D)
    combined = jnp.sum(picked * route_weights[:, :, None], axis=1)
    expert_cols = lax.psum_scatter(
        combined.astype(jnp.bfloat16), "tensor", scatter_dimension=1, tiled=True
    ).astype(jnp.float32)
    return (resid_cols + expert_cols).astype(jnp.bfloat16)


def solution(mesh):
    return jax.shard_map(
        per_device,
        mesh=mesh,
        in_specs=(
            P("seq", None),
            P("seq", "tensor"),
            P("seq", "tensor"),
            P("seq", "tensor"),
            P("seq", "tensor"),
            P("seq", "tensor"),
            P(),
            P(None, "tensor"),
            P("tensor", None),
            P(),
            P("seq", None),
            P("seq", None),
            P(None, None, None, "tensor"),
            P(None, "tensor", None),
        ),
        out_specs=P("seq", "tensor"),
        check_vma=False,
    )
```

```python
import math

import jax
import jax.numpy as jnp
from jax import lax
from jax.experimental import pallas as pl
from jax.experimental.pallas import tpu as pltpu
from jax.sharding import PartitionSpec as P

D = 1024
HEAD_DIM = 64
TOP = 2
CAP = 384
KEY_TILE = 512
ROW_BLOCK = 128


bucket_edges = [edge for edge in range(1, 17)] + [
    math.ceil(16 * 8 ** (level / 16)) for level in range(1, 16)
]
far_edge = bucket_edges[-1]
epsilon = 1e-06
lowest = -1e30


def attn_kernel(scal_ref, dtab_ref, q_ref, k_ref, v_ref, m_in, l_in, acc_in, m_ref, l_ref, acc_ref):
    t = pl.program_id(0)
    tk = k_ref.shape[0]
    rows_all = q_ref.shape[0]

    @pl.when(t == 0)
    def _():
        m_ref[...] = m_in[...]
        l_ref[...] = l_in[...]
        acc_ref[...] = acc_in[...]

    n_valid = scal_ref[2]
    active = (t < n_valid) & ((t < scal_ref[3]) | (t >= scal_ref[4]))
    half_blocks = rows_all // ROW_BLOCK // 2

    def update(r, near, qk_off):
        rows = pl.ds(pl.multiple_of(r * ROW_BLOCK, ROW_BLOCK), ROW_BLOCK)
        q = q_ref[rows, :]
        k = k_ref[...]
        v = v_ref[...]
        lane = lax.broadcasted_iota(jnp.int32, (1, q.shape[1]), 1) < HEAD_DIM
        zero_q = jnp.zeros_like(q)
        if near:
            base = qk_off + r * ROW_BLOCK - t * tk
            d = (
                base
                + lax.broadcasted_iota(jnp.int32, (ROW_BLOCK, tk), 0)
                - lax.broadcasted_iota(jnp.int32, (ROW_BLOCK, tk), 1)
            )
            allowed = d >= 0
            bucket = jnp.zeros(d.shape, jnp.int32)
            for edge in bucket_edges:
                bucket = bucket + (d >= edge).astype(jnp.int32)
        news = []
        alphas = []
        pvs = []
        for h in range(2):
            qh = jnp.where(lane, q, zero_q) if h == 0 else jnp.where(lane, zero_q, q)
            s = lax.dot_general(
                qh, k, (((1,), (1,)), ((), ())), preferred_element_type=jnp.float32
            )
            if near:
                delta = jnp.zeros(s.shape, jnp.float32)
                for level in range(len(bucket_edges)):
                    delta = jnp.where(bucket == level, dtab_ref[level, h], delta)
                s = jnp.where(allowed, s + delta, -jnp.inf)
            m_prev = m_ref[h, rows, :]
            m_curr = jnp.max(s, axis=1, keepdims=True)
            m_next = jnp.maximum(m_prev, m_curr)
            p = jnp.exp(s - jnp.tile(m_next, (1, tk // m_next.shape[1])))
            alpha = jnp.exp(m_prev - m_next)
            l_ref[h, rows, :] = alpha * l_ref[h, rows, :] + jnp.sum(p, axis=1, keepdims=True)
            m_ref[h, rows, :] = m_next
            pv = jnp.dot(p.astype(v.dtype), v, preferred_element_type=jnp.float32)
            alphas.append(alpha)
            pvs.append(pv)
        alpha_b = jnp.where(lane, alphas[0], alphas[1])
        pv_b = jnp.where(lane, pvs[0], pvs[1])
        acc_ref[rows, :] = alpha_b * acc_ref[rows, :] + pv_b

    @pl.when(active)
    def _():
        def one_block(r, carry):
            qk_off = jnp.where(r < half_blocks, scal_ref[0], scal_ref[1])
            dmin = qk_off + r * ROW_BLOCK - (t * tk + tk - 1)
            dmax = qk_off + r * ROW_BLOCK + ROW_BLOCK - 1 - t * tk

            @pl.when(dmin >= far_edge)
            def _():
                update(r, False, qk_off)

            @pl.when((dmin < far_edge) & (dmax >= 0))
            def _():
                update(r, True, qk_off)

            return carry

        lax.fori_loop(0, rows_all // ROW_BLOCK, one_block, 0)


def attend(state, q, pairs, offsets, n_valid, skip, dtab):
    m, l, acc = state
    rows, width = q.shape
    n_tiles = pairs.shape[0] // KEY_TILE
    scal = jnp.stack(
        [jnp.asarray(x, jnp.int32) for x in (offsets[0], offsets[1], n_valid, skip[0], skip[1])]
    )

    def tile_index(t, sc):
        return jnp.maximum(jnp.minimum(t, sc[2] - 1), 0)

    key_map = lambda t, sc: (tile_index(t, sc), 0)
    value_map = lambda t, sc: (tile_index(t, sc), 1)

    full2 = lambda t, sc: (0, 0)
    full3 = lambda t, sc: (0, 0, 0)
    flops = 8 * rows * KEY_TILE * width * n_tiles * 2
    cost = pl.CostEstimate(
        flops=flops,
        transcendentals=2 * rows * KEY_TILE * n_tiles,
        bytes_accessed=pairs.size * 2 + 6 * rows * width * 4,
    )
    return pl.pallas_call(
        attn_kernel,
        out_shape=(
            jax.ShapeDtypeStruct(m.shape, jnp.float32),
            jax.ShapeDtypeStruct(l.shape, jnp.float32),
            jax.ShapeDtypeStruct(acc.shape, jnp.float32),
        ),
        grid_spec=pltpu.PrefetchScalarGridSpec(
            num_scalar_prefetch=1,
            grid=(n_tiles,),
            in_specs=[
                pl.BlockSpec(memory_space=pltpu.SMEM),
                pl.BlockSpec((rows, width), full2),
                pl.BlockSpec((KEY_TILE, width), key_map),
                pl.BlockSpec((KEY_TILE, width), value_map),
                pl.BlockSpec(m.shape, full3),
                pl.BlockSpec(l.shape, full3),
                pl.BlockSpec(acc.shape, full2),
            ],
            out_specs=[
                pl.BlockSpec(m.shape, full3),
                pl.BlockSpec(l.shape, full3),
                pl.BlockSpec(acc.shape, full2),
            ],
        ),
        compiler_params=pltpu.CompilerParams(dimension_semantics=("arbitrary",)),
        cost_estimate=cost,
    )(scal, dtab, q, pairs, pairs, m, l, acc)


def rms_scale(rows, gain):
    return (
        rows * lax.rsqrt(jnp.mean(rows * rows, axis=-1, keepdims=True) + epsilon) * gain
    ).astype(jnp.bfloat16)


def per_device(
    layer_input,
    queries,
    fresh_keys,
    fresh_values,
    cached_keys,
    cached_values,
    start_position,
    bias_table,
    out_weight,
    norm_gain,
    routes,
    route_weights,
    expert_in,
    expert_out,
):
    tok_rows = queries.shape[0]
    width = queries.shape[1]
    half = tok_rows // 2
    offset = start_position[0]
    n_seq = lax.axis_size("seq")
    seq_index = lax.axis_index("seq")
    partner = n_seq - 1 - seq_index
    swap = [(i, n_seq - 1 - i) for i in range(n_seq)]
    rows_q = jnp.concatenate([queries[:half], lax.ppermute(queries[half:], "seq", swap)], 0)
    dtab = bias_table - bias_table[bias_table.shape[0] - 1][None, :]
    state = (
        jnp.full((2, tok_rows, 128), lowest, jnp.float32),
        jnp.zeros((2, tok_rows, 128), jnp.float32),
        jnp.zeros((tok_rows, width), jnp.float32),
    )
    own_tiles = fresh_keys.shape[0] // KEY_TILE
    no_skip = (0, 0)
    own_pairs = jnp.concatenate([fresh_keys, fresh_values], 1)
    state = attend(
        state,
        rows_q,
        own_pairs,
        (0, (partner - seq_index) * tok_rows),
        own_tiles,
        no_skip,
        dtab,
    )
    prior_pairs = lax.all_gather(
        jnp.concatenate([cached_keys, cached_values], 1), "seq", axis=0, tiled=True
    )
    state = attend(
        state,
        rows_q,
        prior_pairs,
        (offset + seq_index * tok_rows, offset + partner * tok_rows),
        prior_pairs.shape[0] // KEY_TILE,
        no_skip,
        dtab,
    )
    all_pairs = lax.all_gather(own_pairs, "seq", axis=0, tiled=True)
    state = attend(
        state,
        rows_q,
        all_pairs,
        (seq_index * tok_rows, partner * tok_rows),
        jnp.maximum(seq_index * own_tiles + own_tiles // 2, (partner + 1) * own_tiles),
        (seq_index * own_tiles, (seq_index + 1) * own_tiles),
        dtab,
    )
    m, l, acc = state
    lane = lax.broadcasted_iota(jnp.int32, (1, width), 1) < HEAD_DIM
    totals = jnp.where(lane, l[0], l[1])
    done_rows = (acc / totals).astype(jnp.bfloat16)
    attended = jnp.concatenate([done_rows[:half], lax.ppermute(done_rows[half:], "seq", swap)], 0)
    attended_full = lax.all_gather(attended, "tensor", axis=1, tiled=True)
    weight_full = lax.all_gather(out_weight, "tensor", axis=0, tiled=True)
    col_width = D // lax.axis_size("tensor")
    col_start = lax.axis_index("tensor") * col_width
    resid = layer_input.astype(jnp.float32) + jnp.dot(
        attended_full, weight_full, preferred_element_type=jnp.float32
    )
    normed = rms_scale(resid, norm_gain)
    resid_cols = lax.dynamic_slice_in_dim(resid, col_start, col_width, 1)
    expert_count = expert_in.shape[0]
    flat_routes = routes.reshape(-1)
    onehot = (flat_routes[:, None] == jnp.arange(expert_count, dtype=jnp.int32)[None, :]).astype(
        jnp.int32
    )
    before = jnp.cumsum(onehot, axis=0) - onehot
    slot = jnp.sum(before * onehot, axis=1)
    target = flat_routes * CAP + slot
    owner = jnp.arange(flat_routes.shape[0], dtype=jnp.int32) // TOP
    slot_owner = jnp.zeros((expert_count * CAP,), jnp.int32).at[target].set(owner)
    buffer = jnp.take(normed, slot_owner, axis=0).reshape(expert_count, CAP, D)
    gate_up = jnp.einsum("ecd,edgf->ecgf", buffer, expert_in, preferred_element_type=jnp.float32)
    hidden = (jax.nn.gelu(gate_up[:, :, 0], approximate=True) * gate_up[:, :, 1]).astype(
        jnp.bfloat16
    )
    expert_rows = jnp.einsum(
        "ecf,efd->ecd", hidden, expert_out, preferred_element_type=jnp.float32
    ).reshape(expert_count * CAP, D)
    picked = jnp.take(expert_rows, target, axis=0).reshape(tok_rows, TOP, D)
    combined = jnp.sum(picked * route_weights[:, :, None], axis=1)
    expert_cols = lax.psum_scatter(
        combined.astype(jnp.bfloat16), "tensor", scatter_dimension=1, tiled=True
    ).astype(jnp.float32)
    return (resid_cols + expert_cols).astype(jnp.bfloat16)


def solution(mesh):
    return jax.shard_map(
        per_device,
        mesh=mesh,
        in_specs=(
            P("seq", None),
            P("seq", "tensor"),
            P("seq", "tensor"),
            P("seq", "tensor"),
            P("seq", "tensor"),
            P("seq", "tensor"),
            P(),
            P(None, "tensor"),
            P("tensor", None),
            P(),
            P("seq", None),
            P("seq", None),
            P(None, None, None, "tensor"),
            P(None, "tensor", None),
        ),
        out_specs=P("seq", "tensor"),
        check_vma=False,
    )
```

```python
import math

import jax
import jax.numpy as jnp
from jax import lax
from jax.experimental import pallas as pl
from jax.experimental.pallas import tpu as pltpu
from jax.sharding import PartitionSpec as P

D = 1024
HEAD_DIM = 64
TOP = 2
CAP = 384
KEY_TILE = 512
ROW_BLOCK = 256


bucket_edges = [edge for edge in range(1, 17)] + [
    math.ceil(16 * 8 ** (level / 16)) for level in range(1, 16)
]
far_edge = bucket_edges[-1]
epsilon = 1e-06
lowest = -1e30


def attn_kernel(scal_ref, dtab_ref, q_ref, k_ref, v_ref, m_in, l_in, acc_in, m_ref, l_ref, acc_ref):
    t = pl.program_id(0)
    tk = k_ref.shape[0]
    rows_all = q_ref.shape[0]

    @pl.when(t == 0)
    def _():
        m_ref[...] = m_in[...]
        l_ref[...] = l_in[...]
        acc_ref[...] = acc_in[...]

    n_valid = scal_ref[2]
    active = (t < n_valid) & ((t < scal_ref[3]) | (t >= scal_ref[4]))
    half_blocks = rows_all // ROW_BLOCK // 2

    def update(r, near, qk_off):
        rows = pl.ds(pl.multiple_of(r * ROW_BLOCK, ROW_BLOCK), ROW_BLOCK)
        q = q_ref[rows, :]
        k = k_ref[...]
        v = v_ref[...]
        lane = lax.broadcasted_iota(jnp.int32, (1, q.shape[1]), 1) < HEAD_DIM
        zero_q = jnp.zeros_like(q)
        if near:
            base = qk_off + r * ROW_BLOCK - t * tk
            d = (
                base
                + lax.broadcasted_iota(jnp.int32, (ROW_BLOCK, tk), 0)
                - lax.broadcasted_iota(jnp.int32, (ROW_BLOCK, tk), 1)
            )
            allowed = d >= 0
            bucket = jnp.zeros(d.shape, jnp.int32)
            for edge in bucket_edges:
                bucket = bucket + (d >= edge).astype(jnp.int32)
        news = []
        alphas = []
        pvs = []
        for h in range(2):
            qh = jnp.where(lane, q, zero_q) if h == 0 else jnp.where(lane, zero_q, q)
            s = lax.dot_general(
                qh, k, (((1,), (1,)), ((), ())), preferred_element_type=jnp.float32
            )
            if near:
                delta = jnp.zeros(s.shape, jnp.float32)
                for level in range(len(bucket_edges)):
                    delta = jnp.where(bucket == level, dtab_ref[level, h], delta)
                s = jnp.where(allowed, s + delta, -jnp.inf)
            m_prev = m_ref[h, rows, :]
            m_curr = jnp.max(s, axis=1, keepdims=True)
            m_next = jnp.maximum(m_prev, m_curr)
            p = jnp.exp(s - jnp.tile(m_next, (1, tk // m_next.shape[1])))
            alpha = jnp.exp(m_prev - m_next)
            l_ref[h, rows, :] = alpha * l_ref[h, rows, :] + jnp.sum(p, axis=1, keepdims=True)
            m_ref[h, rows, :] = m_next
            pv = jnp.dot(p.astype(v.dtype), v, preferred_element_type=jnp.float32)
            alphas.append(alpha)
            pvs.append(pv)
        alpha_b = jnp.where(lane, alphas[0], alphas[1])
        pv_b = jnp.where(lane, pvs[0], pvs[1])
        acc_ref[rows, :] = alpha_b * acc_ref[rows, :] + pv_b

    @pl.when(active)
    def _():
        def one_block(r, carry):
            qk_off = jnp.where(r < half_blocks, scal_ref[0], scal_ref[1])
            dmin = qk_off + r * ROW_BLOCK - (t * tk + tk - 1)
            dmax = qk_off + r * ROW_BLOCK + ROW_BLOCK - 1 - t * tk

            @pl.when(dmin >= far_edge)
            def _():
                update(r, False, qk_off)

            @pl.when((dmin < far_edge) & (dmax >= 0))
            def _():
                update(r, True, qk_off)

            return carry

        lax.fori_loop(0, rows_all // ROW_BLOCK, one_block, 0)


def attend(state, q, pairs, offsets, n_valid, skip, dtab):
    m, l, acc = state
    rows, width = q.shape
    n_tiles = pairs.shape[0] // KEY_TILE
    scal = jnp.stack(
        [jnp.asarray(x, jnp.int32) for x in (offsets[0], offsets[1], n_valid, skip[0], skip[1])]
    )

    def tile_index(t, sc):
        return jnp.maximum(jnp.minimum(t, sc[2] - 1), 0)

    key_map = lambda t, sc: (tile_index(t, sc), 0)
    value_map = lambda t, sc: (tile_index(t, sc), 1)

    full2 = lambda t, sc: (0, 0)
    full3 = lambda t, sc: (0, 0, 0)
    flops = 8 * rows * KEY_TILE * width * n_tiles * 2
    cost = pl.CostEstimate(
        flops=flops,
        transcendentals=2 * rows * KEY_TILE * n_tiles,
        bytes_accessed=pairs.size * 2 + 6 * rows * width * 4,
    )
    return pl.pallas_call(
        attn_kernel,
        out_shape=(
            jax.ShapeDtypeStruct(m.shape, jnp.float32),
            jax.ShapeDtypeStruct(l.shape, jnp.float32),
            jax.ShapeDtypeStruct(acc.shape, jnp.float32),
        ),
        grid_spec=pltpu.PrefetchScalarGridSpec(
            num_scalar_prefetch=1,
            grid=(n_tiles,),
            in_specs=[
                pl.BlockSpec(memory_space=pltpu.SMEM),
                pl.BlockSpec((rows, width), full2),
                pl.BlockSpec((KEY_TILE, width), key_map),
                pl.BlockSpec((KEY_TILE, width), value_map),
                pl.BlockSpec(m.shape, full3),
                pl.BlockSpec(l.shape, full3),
                pl.BlockSpec(acc.shape, full2),
            ],
            out_specs=[
                pl.BlockSpec(m.shape, full3),
                pl.BlockSpec(l.shape, full3),
                pl.BlockSpec(acc.shape, full2),
            ],
        ),
        compiler_params=pltpu.CompilerParams(dimension_semantics=("arbitrary",)),
        cost_estimate=cost,
    )(scal, dtab, q, pairs, pairs, m, l, acc)


def rms_scale(rows, gain):
    return (
        rows * lax.rsqrt(jnp.mean(rows * rows, axis=-1, keepdims=True) + epsilon) * gain
    ).astype(jnp.bfloat16)


def per_device(
    layer_input,
    queries,
    fresh_keys,
    fresh_values,
    cached_keys,
    cached_values,
    start_position,
    bias_table,
    out_weight,
    norm_gain,
    routes,
    route_weights,
    expert_in,
    expert_out,
):
    tok_rows = queries.shape[0]
    width = queries.shape[1]
    half = tok_rows // 2
    offset = start_position[0]
    n_seq = lax.axis_size("seq")
    seq_index = lax.axis_index("seq")
    partner = n_seq - 1 - seq_index
    swap = [(i, n_seq - 1 - i) for i in range(n_seq)]
    rows_q = jnp.concatenate([queries[:half], lax.ppermute(queries[half:], "seq", swap)], 0)
    dtab = bias_table - bias_table[bias_table.shape[0] - 1][None, :]
    state = (
        jnp.full((2, tok_rows, 128), lowest, jnp.float32),
        jnp.zeros((2, tok_rows, 128), jnp.float32),
        jnp.zeros((tok_rows, width), jnp.float32),
    )
    own_tiles = fresh_keys.shape[0] // KEY_TILE
    no_skip = (0, 0)
    own_pairs = jnp.concatenate([fresh_keys, fresh_values], 1)
    state = attend(
        state,
        rows_q,
        own_pairs,
        (0, (partner - seq_index) * tok_rows),
        own_tiles,
        no_skip,
        dtab,
    )
    prior_pairs = lax.all_gather(
        jnp.concatenate([cached_keys, cached_values], 1), "seq", axis=0, tiled=True
    )
    state = attend(
        state,
        rows_q,
        prior_pairs,
        (offset + seq_index * tok_rows, offset + partner * tok_rows),
        prior_pairs.shape[0] // KEY_TILE,
        no_skip,
        dtab,
    )
    all_pairs = lax.all_gather(own_pairs, "seq", axis=0, tiled=True)
    state = attend(
        state,
        rows_q,
        all_pairs,
        (seq_index * tok_rows, partner * tok_rows),
        jnp.maximum(seq_index * own_tiles + own_tiles // 2, (partner + 1) * own_tiles),
        (seq_index * own_tiles, (seq_index + 1) * own_tiles),
        dtab,
    )
    m, l, acc = state
    lane = lax.broadcasted_iota(jnp.int32, (1, width), 1) < HEAD_DIM
    totals = jnp.where(lane, l[0], l[1])
    done_rows = (acc / totals).astype(jnp.bfloat16)
    attended = jnp.concatenate([done_rows[:half], lax.ppermute(done_rows[half:], "seq", swap)], 0)
    attended_full = lax.all_gather(attended, "tensor", axis=1, tiled=True)
    weight_full = lax.all_gather(out_weight, "tensor", axis=0, tiled=True)
    col_width = D // lax.axis_size("tensor")
    col_start = lax.axis_index("tensor") * col_width
    resid = layer_input.astype(jnp.float32) + jnp.dot(
        attended_full, weight_full, preferred_element_type=jnp.float32
    )
    normed = rms_scale(resid, norm_gain)
    resid_cols = lax.dynamic_slice_in_dim(resid, col_start, col_width, 1)
    expert_count = expert_in.shape[0]
    flat_routes = routes.reshape(-1)
    onehot = (flat_routes[:, None] == jnp.arange(expert_count, dtype=jnp.int32)[None, :]).astype(
        jnp.int32
    )
    before = jnp.cumsum(onehot, axis=0) - onehot
    slot = jnp.sum(before * onehot, axis=1)
    target = flat_routes * CAP + slot
    owner = jnp.arange(flat_routes.shape[0], dtype=jnp.int32) // TOP
    slot_owner = jnp.zeros((expert_count * CAP,), jnp.int32).at[target].set(owner)
    buffer = jnp.take(normed, slot_owner, axis=0).reshape(expert_count, CAP, D)
    gate_up = jnp.einsum("ecd,edgf->ecgf", buffer, expert_in, preferred_element_type=jnp.float32)
    hidden = (jax.nn.gelu(gate_up[:, :, 0], approximate=True) * gate_up[:, :, 1]).astype(
        jnp.bfloat16
    )
    expert_rows = jnp.einsum(
        "ecf,efd->ecd", hidden, expert_out, preferred_element_type=jnp.float32
    ).reshape(expert_count * CAP, D)
    picked = jnp.take(expert_rows, target, axis=0).reshape(tok_rows, TOP, D)
    combined = jnp.sum(picked * route_weights[:, :, None], axis=1)
    expert_cols = lax.psum_scatter(
        combined.astype(jnp.bfloat16), "tensor", scatter_dimension=1, tiled=True
    ).astype(jnp.float32)
    return (resid_cols + expert_cols).astype(jnp.bfloat16)


def solution(mesh):
    return jax.shard_map(
        per_device,
        mesh=mesh,
        in_specs=(
            P("seq", None),
            P("seq", "tensor"),
            P("seq", "tensor"),
            P("seq", "tensor"),
            P("seq", "tensor"),
            P("seq", "tensor"),
            P(),
            P(None, "tensor"),
            P("tensor", None),
            P(),
            P("seq", None),
            P("seq", None),
            P(None, None, None, "tensor"),
            P(None, "tensor", None),
        ),
        out_specs=P("seq", "tensor"),
        check_vma=False,
    )
```

```python
import math

import jax
import jax.numpy as jnp
from jax import lax
from jax.experimental import pallas as pl
from jax.experimental.pallas import tpu as pltpu
from jax.sharding import PartitionSpec as P

D = 1024
HEAD_DIM = 64
TOP = 2
CAP = 384
KEY_TILE = 512
ROW_BLOCK = 512


bucket_edges = [edge for edge in range(1, 17)] + [
    math.ceil(16 * 8 ** (level / 16)) for level in range(1, 16)
]
far_edge = bucket_edges[-1]
epsilon = 1e-06
lowest = -1e30


def attn_kernel(scal_ref, dtab_ref, q_ref, k_ref, v_ref, m_in, l_in, acc_in, m_ref, l_ref, acc_ref):
    t = pl.program_id(0)
    tk = k_ref.shape[0]
    rows_all = q_ref.shape[0]

    @pl.when(t == 0)
    def _():
        m_ref[...] = m_in[...]
        l_ref[...] = l_in[...]
        acc_ref[...] = acc_in[...]

    n_valid = scal_ref[2]
    active = (t < n_valid) & ((t < scal_ref[3]) | (t >= scal_ref[4]))
    half_blocks = rows_all // ROW_BLOCK // 2

    def update(r, near, qk_off):
        rows = pl.ds(pl.multiple_of(r * ROW_BLOCK, ROW_BLOCK), ROW_BLOCK)
        q = q_ref[rows, :]
        k = k_ref[...]
        v = v_ref[...]
        lane = lax.broadcasted_iota(jnp.int32, (1, q.shape[1]), 1) < HEAD_DIM
        zero_q = jnp.zeros_like(q)
        if near:
            base = qk_off + r * ROW_BLOCK - t * tk
            d = (
                base
                + lax.broadcasted_iota(jnp.int32, (ROW_BLOCK, tk), 0)
                - lax.broadcasted_iota(jnp.int32, (ROW_BLOCK, tk), 1)
            )
            allowed = d >= 0
            bucket = jnp.zeros(d.shape, jnp.int32)
            for edge in bucket_edges:
                bucket = bucket + (d >= edge).astype(jnp.int32)
        news = []
        alphas = []
        pvs = []
        for h in range(2):
            qh = jnp.where(lane, q, zero_q) if h == 0 else jnp.where(lane, zero_q, q)
            s = lax.dot_general(
                qh, k, (((1,), (1,)), ((), ())), preferred_element_type=jnp.float32
            )
            if near:
                delta = jnp.zeros(s.shape, jnp.float32)
                for level in range(len(bucket_edges)):
                    delta = jnp.where(bucket == level, dtab_ref[level, h], delta)
                s = jnp.where(allowed, s + delta, -jnp.inf)
            m_prev = m_ref[h, rows, :]
            m_curr = jnp.max(s, axis=1, keepdims=True)
            m_next = jnp.maximum(m_prev, m_curr)
            p = jnp.exp(s - jnp.tile(m_next, (1, tk // m_next.shape[1])))
            alpha = jnp.exp(m_prev - m_next)
            l_ref[h, rows, :] = alpha * l_ref[h, rows, :] + jnp.sum(p, axis=1, keepdims=True)
            m_ref[h, rows, :] = m_next
            pv = jnp.dot(p.astype(v.dtype), v, preferred_element_type=jnp.float32)
            alphas.append(alpha)
            pvs.append(pv)
        alpha_b = jnp.where(lane, alphas[0], alphas[1])
        pv_b = jnp.where(lane, pvs[0], pvs[1])
        acc_ref[rows, :] = alpha_b * acc_ref[rows, :] + pv_b

    @pl.when(active)
    def _():
        def one_block(r, carry):
            qk_off = jnp.where(r < half_blocks, scal_ref[0], scal_ref[1])
            dmin = qk_off + r * ROW_BLOCK - (t * tk + tk - 1)
            dmax = qk_off + r * ROW_BLOCK + ROW_BLOCK - 1 - t * tk

            @pl.when(dmin >= far_edge)
            def _():
                update(r, False, qk_off)

            @pl.when((dmin < far_edge) & (dmax >= 0))
            def _():
                update(r, True, qk_off)

            return carry

        lax.fori_loop(0, rows_all // ROW_BLOCK, one_block, 0)


def attend(state, q, pairs, offsets, n_valid, skip, dtab):
    m, l, acc = state
    rows, width = q.shape
    n_tiles = pairs.shape[0] // KEY_TILE
    scal = jnp.stack(
        [jnp.asarray(x, jnp.int32) for x in (offsets[0], offsets[1], n_valid, skip[0], skip[1])]
    )

    def tile_index(t, sc):
        return jnp.maximum(jnp.minimum(t, sc[2] - 1), 0)

    key_map = lambda t, sc: (tile_index(t, sc), 0)
    value_map = lambda t, sc: (tile_index(t, sc), 1)

    full2 = lambda t, sc: (0, 0)
    full3 = lambda t, sc: (0, 0, 0)
    flops = 8 * rows * KEY_TILE * width * n_tiles * 2
    cost = pl.CostEstimate(
        flops=flops,
        transcendentals=2 * rows * KEY_TILE * n_tiles,
        bytes_accessed=pairs.size * 2 + 6 * rows * width * 4,
    )
    return pl.pallas_call(
        attn_kernel,
        out_shape=(
            jax.ShapeDtypeStruct(m.shape, jnp.float32),
            jax.ShapeDtypeStruct(l.shape, jnp.float32),
            jax.ShapeDtypeStruct(acc.shape, jnp.float32),
        ),
        grid_spec=pltpu.PrefetchScalarGridSpec(
            num_scalar_prefetch=1,
            grid=(n_tiles,),
            in_specs=[
                pl.BlockSpec(memory_space=pltpu.SMEM),
                pl.BlockSpec((rows, width), full2),
                pl.BlockSpec((KEY_TILE, width), key_map),
                pl.BlockSpec((KEY_TILE, width), value_map),
                pl.BlockSpec(m.shape, full3),
                pl.BlockSpec(l.shape, full3),
                pl.BlockSpec(acc.shape, full2),
            ],
            out_specs=[
                pl.BlockSpec(m.shape, full3),
                pl.BlockSpec(l.shape, full3),
                pl.BlockSpec(acc.shape, full2),
            ],
        ),
        compiler_params=pltpu.CompilerParams(dimension_semantics=("arbitrary",)),
        cost_estimate=cost,
    )(scal, dtab, q, pairs, pairs, m, l, acc)


def rms_scale(rows, gain):
    return (
        rows * lax.rsqrt(jnp.mean(rows * rows, axis=-1, keepdims=True) + epsilon) * gain
    ).astype(jnp.bfloat16)


def per_device(
    layer_input,
    queries,
    fresh_keys,
    fresh_values,
    cached_keys,
    cached_values,
    start_position,
    bias_table,
    out_weight,
    norm_gain,
    routes,
    route_weights,
    expert_in,
    expert_out,
):
    tok_rows = queries.shape[0]
    width = queries.shape[1]
    half = tok_rows // 2
    offset = start_position[0]
    n_seq = lax.axis_size("seq")
    seq_index = lax.axis_index("seq")
    partner = n_seq - 1 - seq_index
    swap = [(i, n_seq - 1 - i) for i in range(n_seq)]
    rows_q = jnp.concatenate([queries[:half], lax.ppermute(queries[half:], "seq", swap)], 0)
    dtab = bias_table - bias_table[bias_table.shape[0] - 1][None, :]
    state = (
        jnp.full((2, tok_rows, 128), lowest, jnp.float32),
        jnp.zeros((2, tok_rows, 128), jnp.float32),
        jnp.zeros((tok_rows, width), jnp.float32),
    )
    own_tiles = fresh_keys.shape[0] // KEY_TILE
    no_skip = (0, 0)
    own_pairs = jnp.concatenate([fresh_keys, fresh_values], 1)
    state = attend(
        state,
        rows_q,
        own_pairs,
        (0, (partner - seq_index) * tok_rows),
        own_tiles,
        no_skip,
        dtab,
    )
    prior_pairs = lax.all_gather(
        jnp.concatenate([cached_keys, cached_values], 1), "seq", axis=0, tiled=True
    )
    state = attend(
        state,
        rows_q,
        prior_pairs,
        (offset + seq_index * tok_rows, offset + partner * tok_rows),
        prior_pairs.shape[0] // KEY_TILE,
        no_skip,
        dtab,
    )
    all_pairs = lax.all_gather(own_pairs, "seq", axis=0, tiled=True)
    state = attend(
        state,
        rows_q,
        all_pairs,
        (seq_index * tok_rows, partner * tok_rows),
        jnp.maximum(seq_index * own_tiles + own_tiles // 2, (partner + 1) * own_tiles),
        (seq_index * own_tiles, (seq_index + 1) * own_tiles),
        dtab,
    )
    m, l, acc = state
    lane = lax.broadcasted_iota(jnp.int32, (1, width), 1) < HEAD_DIM
    totals = jnp.where(lane, l[0], l[1])
    done_rows = (acc / totals).astype(jnp.bfloat16)
    attended = jnp.concatenate([done_rows[:half], lax.ppermute(done_rows[half:], "seq", swap)], 0)
    attended_full = lax.all_gather(attended, "tensor", axis=1, tiled=True)
    weight_full = lax.all_gather(out_weight, "tensor", axis=0, tiled=True)
    col_width = D // lax.axis_size("tensor")
    col_start = lax.axis_index("tensor") * col_width
    resid = layer_input.astype(jnp.float32) + jnp.dot(
        attended_full, weight_full, preferred_element_type=jnp.float32
    )
    normed = rms_scale(resid, norm_gain)
    resid_cols = lax.dynamic_slice_in_dim(resid, col_start, col_width, 1)
    expert_count = expert_in.shape[0]
    flat_routes = routes.reshape(-1)
    onehot = (flat_routes[:, None] == jnp.arange(expert_count, dtype=jnp.int32)[None, :]).astype(
        jnp.int32
    )
    before = jnp.cumsum(onehot, axis=0) - onehot
    slot = jnp.sum(before * onehot, axis=1)
    target = flat_routes * CAP + slot
    owner = jnp.arange(flat_routes.shape[0], dtype=jnp.int32) // TOP
    slot_owner = jnp.zeros((expert_count * CAP,), jnp.int32).at[target].set(owner)
    buffer = jnp.take(normed, slot_owner, axis=0).reshape(expert_count, CAP, D)
    gate_up = jnp.einsum("ecd,edgf->ecgf", buffer, expert_in, preferred_element_type=jnp.float32)
    hidden = (jax.nn.gelu(gate_up[:, :, 0], approximate=True) * gate_up[:, :, 1]).astype(
        jnp.bfloat16
    )
    expert_rows = jnp.einsum(
        "ecf,efd->ecd", hidden, expert_out, preferred_element_type=jnp.float32
    ).reshape(expert_count * CAP, D)
    picked = jnp.take(expert_rows, target, axis=0).reshape(tok_rows, TOP, D)
    combined = jnp.sum(picked * route_weights[:, :, None], axis=1)
    expert_cols = lax.psum_scatter(
        combined.astype(jnp.bfloat16), "tensor", scatter_dimension=1, tiled=True
    ).astype(jnp.float32)
    return (resid_cols + expert_cols).astype(jnp.bfloat16)


def solution(mesh):
    return jax.shard_map(
        per_device,
        mesh=mesh,
        in_specs=(
            P("seq", None),
            P("seq", "tensor"),
            P("seq", "tensor"),
            P("seq", "tensor"),
            P("seq", "tensor"),
            P("seq", "tensor"),
            P(),
            P(None, "tensor"),
            P("tensor", None),
            P(),
            P("seq", None),
            P("seq", None),
            P(None, None, None, "tensor"),
            P(None, "tensor", None),
        ),
        out_specs=P("seq", "tensor"),
        check_vma=False,
    )
```

```python
import math

import jax
import jax.numpy as jnp
from jax import lax
from jax.experimental import pallas as pl
from jax.experimental.pallas import tpu as pltpu
from jax.sharding import PartitionSpec as P

D = 1024
HEAD_DIM = 64
TOP = 2
CAP = 384
KEY_TILE = 1024
ROW_BLOCK = 512


bucket_edges = [edge for edge in range(1, 17)] + [
    math.ceil(16 * 8 ** (level / 16)) for level in range(1, 16)
]
far_edge = bucket_edges[-1]
epsilon = 1e-06
lowest = -1e30


def attn_kernel(scal_ref, dtab_ref, q_ref, k_ref, v_ref, m_in, l_in, acc_in, m_ref, l_ref, acc_ref):
    t = pl.program_id(0)
    tk = k_ref.shape[0]
    rows_all = q_ref.shape[0]

    @pl.when(t == 0)
    def _():
        m_ref[...] = m_in[...]
        l_ref[...] = l_in[...]
        acc_ref[...] = acc_in[...]

    n_valid = scal_ref[2]
    active = (t < n_valid) & ((t < scal_ref[3]) | (t >= scal_ref[4]))
    half_blocks = rows_all // ROW_BLOCK // 2

    def update(r, near, qk_off):
        rows = pl.ds(pl.multiple_of(r * ROW_BLOCK, ROW_BLOCK), ROW_BLOCK)
        q = q_ref[rows, :]
        k = k_ref[...]
        v = v_ref[...]
        lane = lax.broadcasted_iota(jnp.int32, (1, q.shape[1]), 1) < HEAD_DIM
        zero_q = jnp.zeros_like(q)
        if near:
            base = qk_off + r * ROW_BLOCK - t * tk
            d = (
                base
                + lax.broadcasted_iota(jnp.int32, (ROW_BLOCK, tk), 0)
                - lax.broadcasted_iota(jnp.int32, (ROW_BLOCK, tk), 1)
            )
            allowed = d >= 0
            bucket = jnp.zeros(d.shape, jnp.int32)
            for edge in bucket_edges:
                bucket = bucket + (d >= edge).astype(jnp.int32)
        news = []
        alphas = []
        pvs = []
        for h in range(2):
            qh = jnp.where(lane, q, zero_q) if h == 0 else jnp.where(lane, zero_q, q)
            s = lax.dot_general(
                qh, k, (((1,), (1,)), ((), ())), preferred_element_type=jnp.float32
            )
            if near:
                delta = jnp.zeros(s.shape, jnp.float32)
                for level in range(len(bucket_edges)):
                    delta = jnp.where(bucket == level, dtab_ref[level, h], delta)
                s = jnp.where(allowed, s + delta, -jnp.inf)
            m_prev = m_ref[h, rows, :]
            m_curr = jnp.max(s, axis=1, keepdims=True)
            m_next = jnp.maximum(m_prev, m_curr)
            p = jnp.exp(s - jnp.tile(m_next, (1, tk // m_next.shape[1])))
            alpha = jnp.exp(m_prev - m_next)
            l_ref[h, rows, :] = alpha * l_ref[h, rows, :] + jnp.sum(p, axis=1, keepdims=True)
            m_ref[h, rows, :] = m_next
            pv = jnp.dot(p.astype(v.dtype), v, preferred_element_type=jnp.float32)
            alphas.append(alpha)
            pvs.append(pv)
        alpha_b = jnp.where(lane, alphas[0], alphas[1])
        pv_b = jnp.where(lane, pvs[0], pvs[1])
        acc_ref[rows, :] = alpha_b * acc_ref[rows, :] + pv_b

    @pl.when(active)
    def _():
        def one_block(r, carry):
            qk_off = jnp.where(r < half_blocks, scal_ref[0], scal_ref[1])
            dmin = qk_off + r * ROW_BLOCK - (t * tk + tk - 1)
            dmax = qk_off + r * ROW_BLOCK + ROW_BLOCK - 1 - t * tk

            @pl.when(dmin >= far_edge)
            def _():
                update(r, False, qk_off)

            @pl.when((dmin < far_edge) & (dmax >= 0))
            def _():
                update(r, True, qk_off)

            return carry

        lax.fori_loop(0, rows_all // ROW_BLOCK, one_block, 0)


def attend(state, q, pairs, offsets, n_valid, skip, dtab):
    m, l, acc = state
    rows, width = q.shape
    n_tiles = pairs.shape[0] // KEY_TILE
    scal = jnp.stack(
        [jnp.asarray(x, jnp.int32) for x in (offsets[0], offsets[1], n_valid, skip[0], skip[1])]
    )

    def tile_index(t, sc):
        return jnp.maximum(jnp.minimum(t, sc[2] - 1), 0)

    key_map = lambda t, sc: (tile_index(t, sc), 0)
    value_map = lambda t, sc: (tile_index(t, sc), 1)

    full2 = lambda t, sc: (0, 0)
    full3 = lambda t, sc: (0, 0, 0)
    flops = 8 * rows * KEY_TILE * width * n_tiles * 2
    cost = pl.CostEstimate(
        flops=flops,
        transcendentals=2 * rows * KEY_TILE * n_tiles,
        bytes_accessed=pairs.size * 2 + 6 * rows * width * 4,
    )
    return pl.pallas_call(
        attn_kernel,
        out_shape=(
            jax.ShapeDtypeStruct(m.shape, jnp.float32),
            jax.ShapeDtypeStruct(l.shape, jnp.float32),
            jax.ShapeDtypeStruct(acc.shape, jnp.float32),
        ),
        grid_spec=pltpu.PrefetchScalarGridSpec(
            num_scalar_prefetch=1,
            grid=(n_tiles,),
            in_specs=[
                pl.BlockSpec(memory_space=pltpu.SMEM),
                pl.BlockSpec((rows, width), full2),
                pl.BlockSpec((KEY_TILE, width), key_map),
                pl.BlockSpec((KEY_TILE, width), value_map),
                pl.BlockSpec(m.shape, full3),
                pl.BlockSpec(l.shape, full3),
                pl.BlockSpec(acc.shape, full2),
            ],
            out_specs=[
                pl.BlockSpec(m.shape, full3),
                pl.BlockSpec(l.shape, full3),
                pl.BlockSpec(acc.shape, full2),
            ],
        ),
        compiler_params=pltpu.CompilerParams(dimension_semantics=("arbitrary",)),
        cost_estimate=cost,
    )(scal, dtab, q, pairs, pairs, m, l, acc)


def rms_scale(rows, gain):
    return (
        rows * lax.rsqrt(jnp.mean(rows * rows, axis=-1, keepdims=True) + epsilon) * gain
    ).astype(jnp.bfloat16)


def per_device(
    layer_input,
    queries,
    fresh_keys,
    fresh_values,
    cached_keys,
    cached_values,
    start_position,
    bias_table,
    out_weight,
    norm_gain,
    routes,
    route_weights,
    expert_in,
    expert_out,
):
    tok_rows = queries.shape[0]
    width = queries.shape[1]
    half = tok_rows // 2
    offset = start_position[0]
    n_seq = lax.axis_size("seq")
    seq_index = lax.axis_index("seq")
    partner = n_seq - 1 - seq_index
    swap = [(i, n_seq - 1 - i) for i in range(n_seq)]
    rows_q = jnp.concatenate([queries[:half], lax.ppermute(queries[half:], "seq", swap)], 0)
    dtab = bias_table - bias_table[bias_table.shape[0] - 1][None, :]
    state = (
        jnp.full((2, tok_rows, 128), lowest, jnp.float32),
        jnp.zeros((2, tok_rows, 128), jnp.float32),
        jnp.zeros((tok_rows, width), jnp.float32),
    )
    own_tiles = fresh_keys.shape[0] // KEY_TILE
    no_skip = (0, 0)
    own_pairs = jnp.concatenate([fresh_keys, fresh_values], 1)
    state = attend(
        state,
        rows_q,
        own_pairs,
        (0, (partner - seq_index) * tok_rows),
        own_tiles,
        no_skip,
        dtab,
    )
    prior_pairs = lax.all_gather(
        jnp.concatenate([cached_keys, cached_values], 1), "seq", axis=0, tiled=True
    )
    state = attend(
        state,
        rows_q,
        prior_pairs,
        (offset + seq_index * tok_rows, offset + partner * tok_rows),
        prior_pairs.shape[0] // KEY_TILE,
        no_skip,
        dtab,
    )
    all_pairs = lax.all_gather(own_pairs, "seq", axis=0, tiled=True)
    state = attend(
        state,
        rows_q,
        all_pairs,
        (seq_index * tok_rows, partner * tok_rows),
        jnp.maximum(seq_index * own_tiles + own_tiles // 2, (partner + 1) * own_tiles),
        (seq_index * own_tiles, (seq_index + 1) * own_tiles),
        dtab,
    )
    m, l, acc = state
    lane = lax.broadcasted_iota(jnp.int32, (1, width), 1) < HEAD_DIM
    totals = jnp.where(lane, l[0], l[1])
    done_rows = (acc / totals).astype(jnp.bfloat16)
    attended = jnp.concatenate([done_rows[:half], lax.ppermute(done_rows[half:], "seq", swap)], 0)
    attended_full = lax.all_gather(attended, "tensor", axis=1, tiled=True)
    weight_full = lax.all_gather(out_weight, "tensor", axis=0, tiled=True)
    col_width = D // lax.axis_size("tensor")
    col_start = lax.axis_index("tensor") * col_width
    resid = layer_input.astype(jnp.float32) + jnp.dot(
        attended_full, weight_full, preferred_element_type=jnp.float32
    )
    normed = rms_scale(resid, norm_gain)
    resid_cols = lax.dynamic_slice_in_dim(resid, col_start, col_width, 1)
    expert_count = expert_in.shape[0]
    flat_routes = routes.reshape(-1)
    onehot = (flat_routes[:, None] == jnp.arange(expert_count, dtype=jnp.int32)[None, :]).astype(
        jnp.int32
    )
    before = jnp.cumsum(onehot, axis=0) - onehot
    slot = jnp.sum(before * onehot, axis=1)
    target = flat_routes * CAP + slot
    owner = jnp.arange(flat_routes.shape[0], dtype=jnp.int32) // TOP
    slot_owner = jnp.zeros((expert_count * CAP,), jnp.int32).at[target].set(owner)
    buffer = jnp.take(normed, slot_owner, axis=0).reshape(expert_count, CAP, D)
    gate_up = jnp.einsum("ecd,edgf->ecgf", buffer, expert_in, preferred_element_type=jnp.float32)
    hidden = (jax.nn.gelu(gate_up[:, :, 0], approximate=True) * gate_up[:, :, 1]).astype(
        jnp.bfloat16
    )
    expert_rows = jnp.einsum(
        "ecf,efd->ecd", hidden, expert_out, preferred_element_type=jnp.float32
    ).reshape(expert_count * CAP, D)
    picked = jnp.take(expert_rows, target, axis=0).reshape(tok_rows, TOP, D)
    combined = jnp.sum(picked * route_weights[:, :, None], axis=1)
    expert_cols = lax.psum_scatter(
        combined.astype(jnp.bfloat16), "tensor", scatter_dimension=1, tiled=True
    ).astype(jnp.float32)
    return (resid_cols + expert_cols).astype(jnp.bfloat16)


def solution(mesh):
    return jax.shard_map(
        per_device,
        mesh=mesh,
        in_specs=(
            P("seq", None),
            P("seq", "tensor"),
            P("seq", "tensor"),
            P("seq", "tensor"),
            P("seq", "tensor"),
            P("seq", "tensor"),
            P(),
            P(None, "tensor"),
            P("tensor", None),
            P(),
            P("seq", None),
            P("seq", None),
            P(None, None, None, "tensor"),
            P(None, "tensor", None),
        ),
        out_specs=P("seq", "tensor"),
        check_vma=False,
    )
```
